256 devices in a mesh: gx: 32 (over z, y), gy: 4 (over x), gz: 2 (over core).
Axes of the slice: x: 4, y: 4, z: 8, core: 2. Of those that a mesh axis runs over, the one named last changes fastest.
Arguments:
- mass_per_volume: float32 [16, 512, 512], P('gz', 'gx', 'gy'), may hold values from 0.5 to 2
- flow_speed: float32 [3, 16, 512, 512], P(None, 'gz', 'gx', 'gy'), may hold values from -3 to 3
- pressure: float32 [16, 512, 512], P('gz', 'gx', 'gy'), may hold values from 0.5 to 2
- cotangent: float32 [5, 16, 512, 512], P(None, 'gz', 'gx', 'gy'), may hold values from -6 to 6
- weight_inner: float32 [64, 9], replicated, may hold values from -2 to 2
- weight_middle: float32 [64, 64], replicated, may hold values from -0.75 to 0.75
- weight_outer: float32 [64], replicated, may hold values from -0.75 to 0.75
Outputs:
- state_next: float32 [5, 16, 512, 512], P(None, 'gz', 'gx', 'gy')
- adjoint_density: float32 [16, 512, 512], P('gz', 'gx', 'gy')
- adjoint_velocity: float32 [3, 16, 512, 512], P(None, 'gz', 'gx', 'gy')
- adjoint_pressure: float32 [16, 512, 512], P('gz', 'gx', 'gy')
- adjoint_inner: float32 [64, 9], replicated
- adjoint_middle: float32 [64, 64], replicated
- adjoint_outer: float32 [64], replicated
The draws below stay inside these ranges and needn't reach their ends.
All inputs are finite; a program needn't handle non-finite values.
Results may differ from the reference program's by a relative error of at most 0.0003.
Values sent between devices are 32-bit elements; how exact they have to be, the bound alone decides.
No kernel may reach another device: no remote copies, remote signals or barrier semaphores. Data moves between devices by JAX's collectives and lax.ppermute only.
A program may use at most 64 MiB of HBM per device.

```python
import math
import jax
import jax.numpy as jnp
from jax import lax

HID = 64
NX = 512
NY = 512
NZ = 16


def block_levels(own_key, dims, pieces, smallest, high):
    factor_of = 1.0
    for dim, blocks in pieces:
        heights = jax.random.uniform(jax.random.fold_in(jax.random.fold_in(own_key, 6), dim), (blocks,), jnp.float32, smallest / len(pieces), high / len(pieces))
        factor_of = factor_of * jnp.repeat(jnp.exp(heights), dims[dim] // blocks).reshape((-1,) + (1,) * (len(dims) - 1 - dim))
    return factor_of


def gaussian(own_key, dims, width, limit, pieces=(), kind=jnp.bfloat16):
    array = width * jax.random.normal(own_key, dims, jnp.float32)
    if pieces:
        array = array * block_levels(own_key, dims, pieces, -0.22, 0.18)
    return jnp.clip(array, -limit, limit).astype(kind)


def setup_inputs(seed: int = 0) -> dict:
    keys = jax.random.split(jax.random.key(seed), 8)
    return {
        "mass_per_volume": jnp.clip(0.5 + 1.5 * jax.random.uniform(keys[0], (NZ, NX, NY), jnp.float32) ** block_levels(keys[0], (NZ, NX, NY), ((0, 2), (1, 32), (2, 4)), -0.2, 0.2), 0.5, 2.0),
        "flow_speed": gaussian(keys[1], (3, NZ, NX, NY), 0.5, 3.0, ((1, 2), (2, 32), (3, 4)), jnp.float32),
        "pressure": jnp.clip(0.5 + 1.5 * jax.random.uniform(keys[2], (NZ, NX, NY), jnp.float32) ** block_levels(keys[2], (NZ, NX, NY), ((0, 2), (1, 32), (2, 4)), -0.2, 0.2), 0.5, 2.0),
        "cotangent": gaussian(keys[3], (5, NZ, NX, NY), 1.0, 6.0, ((1, 2), (2, 32), (3, 4)), jnp.float32),
        "weight_inner": gaussian(keys[4], (HID, 9), 9 ** -0.5, 2.0, (), jnp.float32),
        "weight_middle": gaussian(keys[5], (HID, HID), HID ** -0.5, 0.75, (), jnp.float32),
        "weight_outer": gaussian(keys[6], (HID,), HID ** -0.5, 0.75, (), jnp.float32),
    }


HEAT_RATIO = 1.4
THERMAL_DIFFUSE = 3.5
EDDY_SCALE = 0.5
TIME_STEP = 0.1
COMPACT_ALPHA = 1.0 / 3.0
COMPACT_NEAR = 14.0 / 9.0
COMPACT_FAR = 1.0 / 9.0
HIGHEST_PRECISION = lax.Precision.HIGHEST

def prepare(mass_per_volume, flow_speed, pressure):
    energy = pressure / (HEAT_RATIO - 1.0) + 0.5 * mass_per_volume * lax.optimization_barrier(jnp.sum(flow_speed * flow_speed, 0))
    state_now = jnp.concatenate([mass_per_volume[None], mass_per_volume[None] * flow_speed, energy[None]], 0)
    scalars = jnp.concatenate([flow_speed, (pressure / mass_per_volume)[None]], 0)
    return (state_now, scalars)

def fluxes(mass_per_volume, flow_speed, pressure, upstream_cotangent, eddy_viscosity):
    energy = pressure / (HEAT_RATIO - 1.0) + 0.5 * mass_per_volume * lax.optimization_barrier(jnp.sum(flow_speed * flow_speed, 0))
    attenuation_coefficient = mass_per_volume * eddy_viscosity
    stagnation_specific_energy = energy + pressure
    directions = []
    for traversal_axis in range(3):
        transported_array = flow_speed[traversal_axis]
        partition_parts = [mass_per_volume * transported_array]
        for coordinate_slot in range(3):
            mass_flux_array = mass_per_volume * flow_speed[coordinate_slot] * transported_array - attenuation_coefficient * upstream_cotangent[traversal_axis, coordinate_slot]
            if coordinate_slot == traversal_axis:
                mass_flux_array = mass_flux_array + pressure
            partition_parts.append(mass_flux_array)
        partition_parts.append(stagnation_specific_energy * transported_array - THERMAL_DIFFUSE * attenuation_coefficient * upstream_cotangent[traversal_axis, 3])
        directions.append(jnp.stack(partition_parts))
    return jnp.stack(directions)

def derive_x(values):
    spectrum = jnp.fft.rfft(values, axis=-2)
    wavenumber = 2.0 * math.pi * jnp.arange(NX // 2 + 1, dtype=jnp.float32) / NX
    symbol = (COMPACT_NEAR * jnp.sin(wavenumber) + 0.5 * COMPACT_FAR * jnp.sin(2.0 * wavenumber)) / (1.0 + 2.0 * COMPACT_ALPHA * jnp.cos(wavenumber))
    return jnp.fft.irfft(spectrum * (1j * symbol)[:, None], n=NX, axis=-2)

def explicit(values, along_axis):

    def shifted(offset):
        return jnp.roll(values, -offset, axis=along_axis)
    return (45.0 * (shifted(1) - shifted(-1)) - 9.0 * (shifted(2) - shifted(-2)) + (shifted(3) - shifted(-3))) / 60.0

def viscosity(upstream_cotangent, inner_weight, middle_weight, outer_weight):
    features = upstream_cotangent[:, :3].reshape((9,) + upstream_cotangent.shape[2:])
    planes = jnp.moveaxis(features, 1, 0)

    def one_plane(plane_features):
        hidden = jnp.tanh(jnp.einsum('hc,cxy->hxy', inner_weight, plane_features, precision=HIGHEST_PRECISION))
        hidden = jnp.tanh(jnp.einsum('hk,kxy->hxy', middle_weight, hidden, precision=HIGHEST_PRECISION))
        output = jnp.einsum('h,hxy->xy', outer_weight, hidden, precision=HIGHEST_PRECISION)
        return EDDY_SCALE * jax.nn.softplus(output)
    return lax.map(jax.checkpoint(one_plane), planes)

def forward(mass_per_volume, flow_speed, pressure, weight_inner, weight_middle, weight_outer):
    state_now, scalars = prepare(mass_per_volume, flow_speed, pressure)
    gradients = jnp.stack([derive_x(scalars), explicit(scalars, -1), explicit(scalars, -3)])
    eddy_viscosity = viscosity(gradients, weight_inner, weight_middle, weight_outer)
    flux_all = fluxes(mass_per_volume, flow_speed, pressure, gradients, eddy_viscosity)
    divergence = derive_x(flux_all[0]) + explicit(flux_all[1], -1) + explicit(flux_all[2], -3)
    return state_now - TIME_STEP * divergence

def reference(mass_per_volume, flow_speed, pressure, cotangent, weight_inner, weight_middle, weight_outer):
    state_next, pullback = jax.vjp(forward, mass_per_volume, flow_speed, pressure, weight_inner, weight_middle, weight_outer)
    pulled = pullback(cotangent)
    factor = 1.0 / math.sqrt(NX * NY * NZ)
    return (state_next, pulled[0], pulled[1], pulled[2], pulled[3] * factor, pulled[4] * factor, pulled[5] * factor)
```

```python
import math

import jax
import jax.numpy as jnp
import numpy as np
from jax import lax
from jax.sharding import PartitionSpec as P

HEAT_RATIO = 1.4
THERMAL_DIFFUSE = 3.5
EDDY_SCALE = 0.5
TIME_STEP = 0.1
COMPACT_ALPHA = 1.0 / 3.0
COMPACT_NEAR = 14.0 / 9.0
COMPACT_FAR = 1.0 / 9.0
HIGHEST_PRECISION = lax.Precision.HIGHEST
NEAR_HALO = 2
NETWORK_PRECISION = lax.Precision.HIGH


def from_behind(value, axis, steps):
    count = lax.axis_size(axis)
    pairs = [(source, (source + steps) % count) for source in range(count)]
    return lax.ppermute(value, axis, pairs)


def prepare(mass_per_volume, flow_speed, pressure):
    energy = pressure / (HEAT_RATIO - 1.0) + 0.5 * mass_per_volume * jnp.sum(
        flow_speed * flow_speed, 0
    )
    state_now = jnp.concatenate(
        [mass_per_volume[None], mass_per_volume[None] * flow_speed, energy[None]], 0
    )
    scalars = jnp.concatenate([flow_speed, (pressure / mass_per_volume)[None]], 0)
    return (state_now, scalars)


def fluxes(mass_per_volume, flow_speed, pressure, upstream_cotangent, eddy_viscosity):
    energy = pressure / (HEAT_RATIO - 1.0) + 0.5 * mass_per_volume * jnp.sum(
        flow_speed * flow_speed, 0
    )
    attenuation_coefficient = mass_per_volume * eddy_viscosity
    stagnation_specific_energy = energy + pressure
    directions = []
    for traversal_axis in range(3):
        transported_array = flow_speed[traversal_axis]
        partition_parts = [mass_per_volume * transported_array]
        for coordinate_slot in range(3):
            mass_flux_array = (
                mass_per_volume * flow_speed[coordinate_slot] * transported_array
                - attenuation_coefficient * upstream_cotangent[traversal_axis, coordinate_slot]
            )
            if coordinate_slot == traversal_axis:
                mass_flux_array = mass_flux_array + pressure
            partition_parts.append(mass_flux_array)
        partition_parts.append(
            stagnation_specific_energy * transported_array
            - THERMAL_DIFFUSE * attenuation_coefficient * upstream_cotangent[traversal_axis, 3]
        )
        directions.append(jnp.stack(partition_parts))
    return jnp.stack(directions)


def viscosity(upstream_cotangent, inner_weight, middle_weight, outer_weight):
    features = upstream_cotangent[:, :3].reshape((9,) + upstream_cotangent.shape[2:])
    hidden = jnp.tanh(
        jnp.einsum("hc,czxy->hzxy", inner_weight, features, precision=NETWORK_PRECISION)
    )
    hidden = jnp.tanh(
        jnp.einsum("hk,kzxy->hzxy", middle_weight, hidden, precision=NETWORK_PRECISION)
    )
    output = jnp.einsum("h,hzxy->zxy", outer_weight, hidden, precision=NETWORK_PRECISION)
    return EDDY_SCALE * jax.nn.softplus(output)


def local_flux(
    density_in, velocity_in, pressure_in, upstream_cotangent, inner_in, middle_in, outer_in
):
    eddy_viscosity = viscosity(upstream_cotangent, inner_in, middle_in, outer_in)
    return fluxes(density_in, velocity_in, pressure_in, upstream_cotangent, eddy_viscosity)


def compact_tables(x_cells, line_length):
    eye = np.eye(line_length)
    system = eye + COMPACT_ALPHA * (np.roll(eye, 1, 1) + np.roll(eye, -1, 1))
    right = np.zeros((line_length, line_length))
    cells = np.arange(line_length)
    for offset, value in (
        (1, 0.5 * COMPACT_NEAR),
        (-1, -0.5 * COMPACT_NEAR),
        (2, 0.25 * COMPACT_FAR),
        (-2, -0.25 * COMPACT_FAR),
    ):
        right[cells, (cells + offset) % line_length] += value
    row = np.linalg.solve(system, right)[0]

    def coef(offset):
        return row[offset % line_length]

    ratio = (-1.0 + np.sqrt(1.0 - 4.0 * COMPACT_ALPHA**2)) / (2.0 * COMPACT_ALPHA)
    gain = coef(NEAR_HALO + 1) / ratio ** (NEAR_HALO + 1)
    n, h = x_cells, NEAR_HALO
    own = np.arange(n)
    send = np.zeros((2 * h + 4, n))
    for k in range(h):
        send[k, n - h + k] = 1.0
    send[h, : n - h] = ratio ** (n - own[: n - h])
    send[h + 1] = ratio ** (2 * n - own)
    for k in range(h):
        send[h + 2 + k, k] = 1.0
    send[2 * h + 2, h:] = ratio ** own[h:]
    send[2 * h + 3] = ratio ** (n + own)
    width = n + 2 * h + 4
    take = np.zeros((n, width))
    for i in range(n):
        take[i, 0] = -gain * ratio**i
        for k in range(h):
            take[i, 1 + k] = coef(-h + k - i)
        take[i, 1 + h] = -gain * ratio**i
        for m in range(n):
            take[i, 2 + h + m] = coef(m - i)
        for k in range(h):
            take[i, 2 + h + n + k] = coef(n + k - i)
        take[i, 2 + 2 * h + n] = gain * ratio ** (n - i)
        take[i, 3 + 2 * h + n] = gain * ratio ** (n - i)
    return send, take


def derive_x(fields):
    x_cells = fields.shape[2]
    groups = lax.axis_size("gx")
    h = NEAR_HALO
    send, take = compact_tables(x_cells, x_cells * groups)
    send = jnp.asarray(send, jnp.float32)
    take = jnp.asarray(take, jnp.float32)
    planes = jnp.einsum("pj,fzjy->fzpy", send, fields, precision=HIGHEST_PRECISION)
    to_right = planes[:, :, : h + 1]
    to_right2 = planes[:, :, h + 1 : h + 2]
    to_left = planes[:, :, h + 2 : 2 * h + 3]
    to_left2 = planes[:, :, 2 * h + 3 :]
    from_left = from_behind(to_right, "gx", 1)
    from_left2 = from_behind(to_right2, "gx", 2)
    from_right = from_behind(to_left, "gx", -1)
    from_right2 = from_behind(to_left2, "gx", -2)
    received = jnp.concatenate([from_left2, from_left, from_right, from_right2], axis=2)
    take_own = take[:, h + 2 : h + 2 + x_cells]
    take_received = jnp.concatenate([take[:, : h + 2], take[:, h + 2 + x_cells :]], axis=1)
    own_part = jnp.einsum("ij,fzjy->fziy", take_own, fields, precision=HIGHEST_PRECISION)
    return own_part + jnp.einsum(
        "ij,fzjy->fziy", take_received, received, precision=HIGHEST_PRECISION
    )


def halo(block, axis, dim, width):
    count = lax.axis_size(axis)
    size = block.shape[dim]
    low_part = lax.slice_in_dim(block, size - width, size, axis=dim)
    high_part = lax.slice_in_dim(block, 0, width, axis=dim)
    if count == 2:
        both = from_behind(jnp.concatenate([low_part, high_part], axis=dim), axis, 1)
        low = lax.slice_in_dim(both, 0, width, axis=dim)
        high = lax.slice_in_dim(both, width, 2 * width, axis=dim)
    else:
        low = from_behind(low_part, axis, 1)
        high = from_behind(high_part, axis, -1)
    return jnp.concatenate([low, block, high], axis=dim)


def centered(extended, along_axis, margin, length):

    def shifted(offset):
        return lax.slice_in_dim(
            extended, margin + offset, margin + offset + length, axis=along_axis
        )

    return (
        45.0 * (shifted(1) - shifted(-1))
        - 9.0 * (shifted(2) - shifted(-2))
        + (shifted(3) - shifted(-3))
    ) / 60.0


def derive_y(fields):
    return centered(halo(fields, "gy", 3, 3), 3, 3, fields.shape[3])


def derive_z(fields):
    return centered(halo(fields, "gz", 1, 3), 1, 3, fields.shape[1])


def butterfly_sum(value, axis):
    count = lax.axis_size(axis)
    step = 1
    while step < count:
        if count % (2 * step) == 0:
            pairs = [(s, s ^ step) for s in range(count)]
            value = value + lax.ppermute(value, axis, pairs)
            step *= 2
        else:
            return lax.psum(value, axis)
    return value


def local(
    mass_per_volume, flow_speed, pressure, cotangent, weight_inner, weight_middle, weight_outer
):
    (state_now, scalars), prepare_pullback = jax.vjp(prepare, mass_per_volume, flow_speed, pressure)
    count = scalars.shape[0]
    first = jnp.concatenate([scalars, cotangent], 0)
    first_x = derive_x(first)
    first_y = derive_y(first)
    first_z = derive_z(first)
    gradients = jnp.stack([first_x[:count], first_y[:count], first_z[:count]])
    spread = jnp.stack([first_x[count:], first_y[count:], first_z[count:]])
    flux_all, flux_pullback = jax.vjp(
        local_flux,
        mass_per_volume,
        flow_speed,
        pressure,
        gradients,
        weight_inner,
        weight_middle,
        weight_outer,
    )
    pulled = flux_pullback(TIME_STEP * spread)
    gradient_bar = pulled[3]
    second_x = derive_x(jnp.concatenate([flux_all[0], gradient_bar[0]], 0))
    second_y = derive_y(jnp.concatenate([flux_all[1], gradient_bar[1]], 0))
    second_z = derive_z(jnp.concatenate([flux_all[2], gradient_bar[2]], 0))
    second = second_x + second_y + second_z
    states = state_now.shape[0]
    state_next = state_now - TIME_STEP * second[:states]
    scalar_bar = -second[states:]
    direct = prepare_pullback((cotangent, scalar_bar))
    weights = (pulled[4], pulled[5], pulled[6])
    flat = jnp.concatenate([w.reshape(-1) for w in weights])
    for axis in ("gz", "gy", "gx"):
        flat = butterfly_sum(flat, axis)
    cells_all = (
        mass_per_volume.size * lax.axis_size("gx") * lax.axis_size("gy") * lax.axis_size("gz")
    )
    factor = 1.0 / math.sqrt(cells_all)
    totals = []
    start = 0
    for w in weights:
        totals.append(flat[start : start + w.size].reshape(w.shape) * factor)
        start += w.size
    return (
        state_next,
        direct[0] + pulled[0],
        direct[1] + pulled[1],
        direct[2] + pulled[2],
        totals[0],
        totals[1],
        totals[2],
    )


def solution(mesh):
    placed = (
        P("gz", "gx", "gy"),
        P(None, "gz", "gx", "gy"),
        P("gz", "gx", "gy"),
        P(None, "gz", "gx", "gy"),
        P(),
        P(),
        P(),
    )
    return jax.shard_map(
        local,
        mesh=mesh,
        in_specs=placed,
        out_specs=(
            P(None, "gz", "gx", "gy"),
            P("gz", "gx", "gy"),
            P(None, "gz", "gx", "gy"),
            P("gz", "gx", "gy"),
            P(),
            P(),
            P(),
        ),
        check_vma=False,
    )
```

```python
import math

import jax
import jax.numpy as jnp
import numpy as np
from jax import lax
from jax.sharding import PartitionSpec as P

HEAT_RATIO = 1.4
THERMAL_DIFFUSE = 3.5
EDDY_SCALE = 0.5
TIME_STEP = 0.1
COMPACT_ALPHA = 1.0 / 3.0
COMPACT_NEAR = 14.0 / 9.0
COMPACT_FAR = 1.0 / 9.0
HIGHEST_PRECISION = lax.Precision.HIGHEST
NEAR_HALO = 2
NETWORK_PRECISION = lax.Precision.HIGH


def from_behind(value, axis, steps):
    count = lax.axis_size(axis)
    pairs = [(source, (source + steps) % count) for source in range(count)]
    return lax.ppermute(value, axis, pairs)


def prepare(mass_per_volume, flow_speed, pressure):
    energy = pressure / (HEAT_RATIO - 1.0) + 0.5 * mass_per_volume * jnp.sum(
        flow_speed * flow_speed, 0
    )
    state_now = jnp.concatenate(
        [mass_per_volume[None], mass_per_volume[None] * flow_speed, energy[None]], 0
    )
    scalars = jnp.concatenate([flow_speed, (pressure / mass_per_volume)[None]], 0)
    return (state_now, scalars)


def fluxes(mass_per_volume, flow_speed, pressure, upstream_cotangent, eddy_viscosity):
    energy = pressure / (HEAT_RATIO - 1.0) + 0.5 * mass_per_volume * jnp.sum(
        flow_speed * flow_speed, 0
    )
    attenuation_coefficient = mass_per_volume * eddy_viscosity
    stagnation_specific_energy = energy + pressure
    directions = []
    for traversal_axis in range(3):
        transported_array = flow_speed[traversal_axis]
        partition_parts = [mass_per_volume * transported_array]
        for coordinate_slot in range(3):
            mass_flux_array = (
                mass_per_volume * flow_speed[coordinate_slot] * transported_array
                - attenuation_coefficient * upstream_cotangent[traversal_axis, coordinate_slot]
            )
            if coordinate_slot == traversal_axis:
                mass_flux_array = mass_flux_array + pressure
            partition_parts.append(mass_flux_array)
        partition_parts.append(
            stagnation_specific_energy * transported_array
            - THERMAL_DIFFUSE * attenuation_coefficient * upstream_cotangent[traversal_axis, 3]
        )
        directions.append(jnp.stack(partition_parts))
    return jnp.stack(directions)


def viscosity(upstream_cotangent, inner_weight, middle_weight, outer_weight):
    features = upstream_cotangent[:, :3].reshape((9,) + upstream_cotangent.shape[2:])
    hidden = jnp.tanh(
        jnp.einsum("hc,czxy->hzxy", inner_weight, features, precision=NETWORK_PRECISION)
    )
    hidden = jnp.tanh(
        jnp.einsum("hk,kzxy->hzxy", middle_weight, hidden, precision=NETWORK_PRECISION)
    )
    output = jnp.einsum("h,hzxy->zxy", outer_weight, hidden, precision=NETWORK_PRECISION)
    return EDDY_SCALE * jax.nn.softplus(output)


def local_flux(
    density_in, velocity_in, pressure_in, upstream_cotangent, inner_in, middle_in, outer_in
):
    eddy_viscosity = viscosity(upstream_cotangent, inner_in, middle_in, outer_in)
    return fluxes(density_in, velocity_in, pressure_in, upstream_cotangent, eddy_viscosity)


def compact_tables(x_cells, line_length):
    eye = np.eye(line_length)
    system = eye + COMPACT_ALPHA * (np.roll(eye, 1, 1) + np.roll(eye, -1, 1))
    right = np.zeros((line_length, line_length))
    cells = np.arange(line_length)
    for offset, value in (
        (1, 0.5 * COMPACT_NEAR),
        (-1, -0.5 * COMPACT_NEAR),
        (2, 0.25 * COMPACT_FAR),
        (-2, -0.25 * COMPACT_FAR),
    ):
        right[cells, (cells + offset) % line_length] += value
    row = np.linalg.solve(system, right)[0]

    def coef(offset):
        return row[offset % line_length]

    ratio = (-1.0 + np.sqrt(1.0 - 4.0 * COMPACT_ALPHA**2)) / (2.0 * COMPACT_ALPHA)
    gain = coef(NEAR_HALO + 1) / ratio ** (NEAR_HALO + 1)
    n, h = x_cells, NEAR_HALO
    own = np.arange(n)
    send = np.zeros((2 * h + 4, n))
    for k in range(h):
        send[k, n - h + k] = 1.0
    send[h, : n - h] = ratio ** (n - own[: n - h])
    send[h + 1] = ratio ** (2 * n - own)
    for k in range(h):
        send[h + 2 + k, k] = 1.0
    send[2 * h + 2, h:] = ratio ** own[h:]
    send[2 * h + 3] = ratio ** (n + own)
    width = n + 2 * h + 4
    take = np.zeros((n, width))
    for i in range(n):
        take[i, 0] = -gain * ratio**i
        for k in range(h):
            take[i, 1 + k] = coef(-h + k - i)
        take[i, 1 + h] = -gain * ratio**i
        for m in range(n):
            take[i, 2 + h + m] = coef(m - i)
        for k in range(h):
            take[i, 2 + h + n + k] = coef(n + k - i)
        take[i, 2 + 2 * h + n] = gain * ratio ** (n - i)
        take[i, 3 + 2 * h + n] = gain * ratio ** (n - i)
    return send, take


def x_send(fields):
    x_cells = fields.shape[2]
    h = NEAR_HALO
    send, _ = compact_tables(x_cells, x_cells * lax.axis_size("gx"))
    send = jnp.asarray(send, jnp.float32)
    planes = jnp.einsum("pj,fzjy->fzpy", send, fields, precision=HIGHEST_PRECISION)
    return (
        planes[:, :, : h + 1],
        planes[:, :, h + 1 : h + 2],
        planes[:, :, h + 2 : 2 * h + 3],
        planes[:, :, 2 * h + 3 :],
    )


def x_exchange(sent):
    to_right, to_right2, to_left, to_left2 = sent
    return (
        from_behind(to_right2, "gx", 2),
        from_behind(to_right, "gx", 1),
        from_behind(to_left, "gx", -1),
        from_behind(to_left2, "gx", -2),
    )


def x_finish(fields, sent, exchange=x_exchange):
    x_cells = fields.shape[2]
    h = NEAR_HALO
    _, take = compact_tables(x_cells, x_cells * lax.axis_size("gx"))
    take = jnp.asarray(take, jnp.float32)
    received = jnp.concatenate(exchange(sent), axis=2)
    take_own = take[:, h + 2 : h + 2 + x_cells]
    take_received = jnp.concatenate([take[:, : h + 2], take[:, h + 2 + x_cells :]], axis=1)
    own_part = jnp.einsum("ij,fzjy->fziy", take_own, fields, precision=HIGHEST_PRECISION)
    return own_part + jnp.einsum(
        "ij,fzjy->fziy", take_received, received, precision=HIGHEST_PRECISION
    )


def derive_x(fields):
    return x_finish(fields, x_send(fields))


def edge_send(block, axis, dim, width):
    size = block.shape[dim]
    low_part = lax.slice_in_dim(block, size - width, size, axis=dim)
    high_part = lax.slice_in_dim(block, 0, width, axis=dim)
    if lax.axis_size(axis) == 2:
        return (jnp.concatenate([low_part, high_part], axis=dim),)
    return (low_part, high_part)


def edge_exchange(sent, axis):
    if len(sent) == 1:
        return (from_behind(sent[0], axis, 1),)
    return (from_behind(sent[0], axis, 1), from_behind(sent[1], axis, -1))


def edge_combine(block, received, dim, width):
    if len(received) == 1:
        low = lax.slice_in_dim(received[0], 0, width, axis=dim)
        high = lax.slice_in_dim(received[0], width, 2 * width, axis=dim)
    else:
        low, high = received
    return jnp.concatenate([low, block, high], axis=dim)


def edge_finish(block, sent, axis, dim, width):
    return edge_combine(block, edge_exchange(sent, axis), dim, width)


def halo(block, axis, dim, width):
    return edge_finish(block, edge_send(block, axis, dim, width), axis, dim, width)


def centered(extended, along_axis, margin, length):

    def shifted(offset):
        return lax.slice_in_dim(
            extended, margin + offset, margin + offset + length, axis=along_axis
        )

    return (
        45.0 * (shifted(1) - shifted(-1))
        - 9.0 * (shifted(2) - shifted(-2))
        + (shifted(3) - shifted(-3))
    ) / 60.0


def derive_y(fields):
    return centered(halo(fields, "gy", 3, 3), 3, 3, fields.shape[3])


def derive_z(fields):
    return centered(halo(fields, "gz", 1, 3), 1, 3, fields.shape[1])


def butterfly_sum(value, axis):
    count = lax.axis_size(axis)
    step = 1
    while step < count:
        if count % (2 * step) == 0:
            pairs = [(s, s ^ step) for s in range(count)]
            value = value + lax.ppermute(value, axis, pairs)
            step *= 2
        else:
            return lax.psum(value, axis)
    return value


def local(
    mass_per_volume, flow_speed, pressure, cotangent, weight_inner, weight_middle, weight_outer
):
    (state_now, scalars), prepare_pullback = jax.vjp(prepare, mass_per_volume, flow_speed, pressure)
    count = scalars.shape[0]
    first = jnp.concatenate([scalars, cotangent], 0)
    first_x = derive_x(first)
    first_y = derive_y(first)
    first_z = derive_z(first)
    gradients = jnp.stack([first_x[:count], first_y[:count], first_z[:count]])
    spread = jnp.stack([first_x[count:], first_y[count:], first_z[count:]])
    flux_all, flux_pullback = jax.vjp(
        local_flux,
        mass_per_volume,
        flow_speed,
        pressure,
        gradients,
        weight_inner,
        weight_middle,
        weight_outer,
    )
    pulled = flux_pullback(TIME_STEP * spread)
    gradient_bar = pulled[3]
    along_x = jnp.concatenate([flux_all[0], gradient_bar[0]], 0)
    along_y = jnp.concatenate([flux_all[1], gradient_bar[1]], 0)
    along_z = jnp.concatenate([flux_all[2], gradient_bar[2]], 0)
    weights = (pulled[4], pulled[5], pulled[6])
    flat = jnp.concatenate([w.reshape(-1) for w in weights])
    got_x = x_exchange(x_send(along_x))
    got_y = edge_exchange(edge_send(along_y, "gy", 3, 3), "gy")
    got_z = edge_exchange(edge_send(along_z, "gz", 1, 3), "gz")
    got_x, got_y, got_z, flat = lax.optimization_barrier((got_x, got_y, got_z, flat))
    second_x = x_finish(along_x, got_x, exchange=lambda received: received)
    second_y = centered(edge_combine(along_y, got_y, 3, 3), 3, 3, along_y.shape[3])
    second_z = centered(edge_combine(along_z, got_z, 1, 3), 1, 3, along_z.shape[1])
    second = second_x + second_y + second_z
    states = state_now.shape[0]
    state_next = state_now - TIME_STEP * second[:states]
    scalar_bar = -second[states:]
    direct = prepare_pullback((cotangent, scalar_bar))
    for axis in ("gz", "gy", "gx"):
        flat = butterfly_sum(flat, axis)
    cells_all = (
        mass_per_volume.size * lax.axis_size("gx") * lax.axis_size("gy") * lax.axis_size("gz")
    )
    factor = 1.0 / math.sqrt(cells_all)
    totals = []
    start = 0
    for w in weights:
        totals.append(flat[start : start + w.size].reshape(w.shape) * factor)
        start += w.size
    return (
        state_next,
        direct[0] + pulled[0],
        direct[1] + pulled[1],
        direct[2] + pulled[2],
        totals[0],
        totals[1],
        totals[2],
    )


def solution(mesh):
    placed = (
        P("gz", "gx", "gy"),
        P(None, "gz", "gx", "gy"),
        P("gz", "gx", "gy"),
        P(None, "gz", "gx", "gy"),
        P(),
        P(),
        P(),
    )
    return jax.shard_map(
        local,
        mesh=mesh,
        in_specs=placed,
        out_specs=(
            P(None, "gz", "gx", "gy"),
            P("gz", "gx", "gy"),
            P(None, "gz", "gx", "gy"),
            P("gz", "gx", "gy"),
            P(),
            P(),
            P(),
        ),
        check_vma=False,
    )
```

```python
import math

import jax
import jax.numpy as jnp
import numpy as np
from jax import lax
from jax.sharding import PartitionSpec as P

HEAT_RATIO = 1.4
THERMAL_DIFFUSE = 3.5
EDDY_SCALE = 0.5
TIME_STEP = 0.1
COMPACT_ALPHA = 1.0 / 3.0
COMPACT_NEAR = 14.0 / 9.0
COMPACT_FAR = 1.0 / 9.0
HIGHEST_PRECISION = lax.Precision.HIGHEST
NEAR_HALO = 2
NETWORK_PRECISION = lax.Precision.HIGH
OFFLOADED_SUM_SIZE = 16384


def from_behind(value, axis, steps):
    count = lax.axis_size(axis)
    pairs = [(source, (source + steps) % count) for source in range(count)]
    return lax.ppermute(value, axis, pairs)


def prepare(mass_per_volume, flow_speed, pressure):
    energy = pressure / (HEAT_RATIO - 1.0) + 0.5 * mass_per_volume * jnp.sum(
        flow_speed * flow_speed, 0
    )
    state_now = jnp.concatenate(
        [mass_per_volume[None], mass_per_volume[None] * flow_speed, energy[None]], 0
    )
    scalars = jnp.concatenate([flow_speed, (pressure / mass_per_volume)[None]], 0)
    return (state_now, scalars)


def fluxes(mass_per_volume, flow_speed, pressure, upstream_cotangent, eddy_viscosity):
    energy = pressure / (HEAT_RATIO - 1.0) + 0.5 * mass_per_volume * jnp.sum(
        flow_speed * flow_speed, 0
    )
    attenuation_coefficient = mass_per_volume * eddy_viscosity
    stagnation_specific_energy = energy + pressure
    directions = []
    for traversal_axis in range(3):
        transported_array = flow_speed[traversal_axis]
        partition_parts = [mass_per_volume * transported_array]
        for coordinate_slot in range(3):
            mass_flux_array = (
                mass_per_volume * flow_speed[coordinate_slot] * transported_array
                - attenuation_coefficient * upstream_cotangent[traversal_axis, coordinate_slot]
            )
            if coordinate_slot == traversal_axis:
                mass_flux_array = mass_flux_array + pressure
            partition_parts.append(mass_flux_array)
        partition_parts.append(
            stagnation_specific_energy * transported_array
            - THERMAL_DIFFUSE * attenuation_coefficient * upstream_cotangent[traversal_axis, 3]
        )
        directions.append(jnp.stack(partition_parts))
    return jnp.stack(directions)


def viscosity(upstream_cotangent, inner_weight, middle_weight, outer_weight):
    features = upstream_cotangent[:, :3].reshape((9,) + upstream_cotangent.shape[2:])
    hidden = jnp.tanh(
        jnp.einsum("hc,czxy->hzxy", inner_weight, features, precision=NETWORK_PRECISION)
    )
    hidden = jnp.tanh(
        jnp.einsum("hk,kzxy->hzxy", middle_weight, hidden, precision=NETWORK_PRECISION)
    )
    output = jnp.einsum("h,hzxy->zxy", outer_weight, hidden, precision=NETWORK_PRECISION)
    return EDDY_SCALE * jax.nn.softplus(output)


def local_flux(
    density_in, velocity_in, pressure_in, upstream_cotangent, inner_in, middle_in, outer_in
):
    eddy_viscosity = viscosity(upstream_cotangent, inner_in, middle_in, outer_in)
    return fluxes(density_in, velocity_in, pressure_in, upstream_cotangent, eddy_viscosity)


def compact_tables(x_cells, line_length):
    eye = np.eye(line_length)
    system = eye + COMPACT_ALPHA * (np.roll(eye, 1, 1) + np.roll(eye, -1, 1))
    right = np.zeros((line_length, line_length))
    cells = np.arange(line_length)
    for offset, value in (
        (1, 0.5 * COMPACT_NEAR),
        (-1, -0.5 * COMPACT_NEAR),
        (2, 0.25 * COMPACT_FAR),
        (-2, -0.25 * COMPACT_FAR),
    ):
        right[cells, (cells + offset) % line_length] += value
    row = np.linalg.solve(system, right)[0]

    def coef(offset):
        return row[offset % line_length]

    ratio = (-1.0 + np.sqrt(1.0 - 4.0 * COMPACT_ALPHA**2)) / (2.0 * COMPACT_ALPHA)
    gain = coef(NEAR_HALO + 1) / ratio ** (NEAR_HALO + 1)
    n, h = x_cells, NEAR_HALO
    own = np.arange(n)
    send = np.zeros((2 * h + 4, n))
    for k in range(h):
        send[k, n - h + k] = 1.0
    send[h, : n - h] = ratio ** (n - own[: n - h])
    send[h + 1] = ratio ** (2 * n - own)
    for k in range(h):
        send[h + 2 + k, k] = 1.0
    send[2 * h + 2, h:] = ratio ** own[h:]
    send[2 * h + 3] = ratio ** (n + own)
    width = n + 2 * h + 4
    take = np.zeros((n, width))
    for i in range(n):
        take[i, 0] = -gain * ratio**i
        for k in range(h):
            take[i, 1 + k] = coef(-h + k - i)
        take[i, 1 + h] = -gain * ratio**i
        for m in range(n):
            take[i, 2 + h + m] = coef(m - i)
        for k in range(h):
            take[i, 2 + h + n + k] = coef(n + k - i)
        take[i, 2 + 2 * h + n] = gain * ratio ** (n - i)
        take[i, 3 + 2 * h + n] = gain * ratio ** (n - i)
    return send, take


def derive_x(fields):
    x_cells = fields.shape[2]
    groups = lax.axis_size("gx")
    h = NEAR_HALO
    send, take = compact_tables(x_cells, x_cells * groups)
    send = jnp.asarray(send, jnp.float32)
    take = jnp.asarray(take, jnp.float32)
    planes = jnp.einsum("pj,fzjy->fzpy", send, fields, precision=HIGHEST_PRECISION)
    to_right = planes[:, :, : h + 1]
    to_right2 = planes[:, :, h + 1 : h + 2]
    to_left = planes[:, :, h + 2 : 2 * h + 3]
    to_left2 = planes[:, :, 2 * h + 3 :]
    from_left = from_behind(to_right, "gx", 1)
    from_left2 = from_behind(to_right2, "gx", 2)
    from_right = from_behind(to_left, "gx", -1)
    from_right2 = from_behind(to_left2, "gx", -2)
    received = jnp.concatenate([from_left2, from_left, from_right, from_right2], axis=2)
    take_own = take[:, h + 2 : h + 2 + x_cells]
    take_received = jnp.concatenate([take[:, : h + 2], take[:, h + 2 + x_cells :]], axis=1)
    own_part = jnp.einsum("ij,fzjy->fziy", take_own, fields, precision=HIGHEST_PRECISION)
    return own_part + jnp.einsum(
        "ij,fzjy->fziy", take_received, received, precision=HIGHEST_PRECISION
    )


def halo(block, axis, dim, width):
    count = lax.axis_size(axis)
    size = block.shape[dim]
    low_part = lax.slice_in_dim(block, size - width, size, axis=dim)
    high_part = lax.slice_in_dim(block, 0, width, axis=dim)
    if count == 2:
        both = from_behind(jnp.concatenate([low_part, high_part], axis=dim), axis, 1)
        low = lax.slice_in_dim(both, 0, width, axis=dim)
        high = lax.slice_in_dim(both, width, 2 * width, axis=dim)
    else:
        low = from_behind(low_part, axis, 1)
        high = from_behind(high_part, axis, -1)
    return jnp.concatenate([low, block, high], axis=dim)


def centered(extended, along_axis, margin, length):

    def shifted(offset):
        return lax.slice_in_dim(
            extended, margin + offset, margin + offset + length, axis=along_axis
        )

    return (
        45.0 * (shifted(1) - shifted(-1))
        - 9.0 * (shifted(2) - shifted(-2))
        + (shifted(3) - shifted(-3))
    ) / 60.0


def derive_y(fields):
    return centered(halo(fields, "gy", 3, 3), 3, 3, fields.shape[3])


def derive_z(fields):
    return centered(halo(fields, "gz", 1, 3), 1, 3, fields.shape[1])


def local(
    mass_per_volume, flow_speed, pressure, cotangent, weight_inner, weight_middle, weight_outer
):
    (state_now, scalars), prepare_pullback = jax.vjp(prepare, mass_per_volume, flow_speed, pressure)
    count = scalars.shape[0]
    first = jnp.concatenate([scalars, cotangent], 0)
    first_x = derive_x(first)
    first_y = derive_y(first)
    first_z = derive_z(first)
    gradients = jnp.stack([first_x[:count], first_y[:count], first_z[:count]])
    spread = jnp.stack([first_x[count:], first_y[count:], first_z[count:]])
    flux_all, flux_pullback = jax.vjp(
        local_flux,
        mass_per_volume,
        flow_speed,
        pressure,
        gradients,
        weight_inner,
        weight_middle,
        weight_outer,
    )
    pulled = flux_pullback(TIME_STEP * spread)
    gradient_bar = pulled[3]
    second_x = derive_x(jnp.concatenate([flux_all[0], gradient_bar[0]], 0))
    second_y = derive_y(jnp.concatenate([flux_all[1], gradient_bar[1]], 0))
    second_z = derive_z(jnp.concatenate([flux_all[2], gradient_bar[2]], 0))
    second = second_x + second_y + second_z
    states = state_now.shape[0]
    state_next = state_now - TIME_STEP * second[:states]
    scalar_bar = -second[states:]
    direct = prepare_pullback((cotangent, scalar_bar))
    weights = (pulled[4], pulled[5], pulled[6])
    flat = jnp.concatenate([w.reshape(-1) for w in weights])
    padded = max(flat.size, OFFLOADED_SUM_SIZE)
    flat = lax.psum(jnp.pad(flat, (0, padded - flat.size)), ("gx", "gy", "gz"))
    cells_all = (
        mass_per_volume.size * lax.axis_size("gx") * lax.axis_size("gy") * lax.axis_size("gz")
    )
    factor = 1.0 / math.sqrt(cells_all)
    totals = []
    start = 0
    for w in weights:
        totals.append(flat[start : start + w.size].reshape(w.shape) * factor)
        start += w.size
    return (
        state_next,
        direct[0] + pulled[0],
        direct[1] + pulled[1],
        direct[2] + pulled[2],
        totals[0],
        totals[1],
        totals[2],
    )


def solution(mesh):
    placed = (
        P("gz", "gx", "gy"),
        P(None, "gz", "gx", "gy"),
        P("gz", "gx", "gy"),
        P(None, "gz", "gx", "gy"),
        P(),
        P(),
        P(),
    )
    return jax.shard_map(
        local,
        mesh=mesh,
        in_specs=placed,
        out_specs=(
            P(None, "gz", "gx", "gy"),
            P("gz", "gx", "gy"),
            P(None, "gz", "gx", "gy"),
            P("gz", "gx", "gy"),
            P(),
            P(),
            P(),
        ),
        check_vma=False,
    )
```

```python
import math

import jax
import jax.numpy as jnp
import numpy as np
from jax import lax
from jax.sharding import PartitionSpec as P

HEAT_RATIO = 1.4
THERMAL_DIFFUSE = 3.5
EDDY_SCALE = 0.5
TIME_STEP = 0.1
COMPACT_ALPHA = 1.0 / 3.0
COMPACT_NEAR = 14.0 / 9.0
COMPACT_FAR = 1.0 / 9.0
HIGHEST_PRECISION = lax.Precision.HIGHEST
NEAR_HALO = 2
NETWORK_PRECISION = lax.Precision.HIGH
LATE_SUM_STEPS = 3


def from_behind(value, axis, steps):
    count = lax.axis_size(axis)
    pairs = [(source, (source + steps) % count) for source in range(count)]
    return lax.ppermute(value, axis, pairs)


def prepare(mass_per_volume, flow_speed, pressure):
    energy = pressure / (HEAT_RATIO - 1.0) + 0.5 * mass_per_volume * jnp.sum(
        flow_speed * flow_speed, 0
    )
    state_now = jnp.concatenate(
        [mass_per_volume[None], mass_per_volume[None] * flow_speed, energy[None]], 0
    )
    scalars = jnp.concatenate([flow_speed, (pressure / mass_per_volume)[None]], 0)
    return (state_now, scalars)


def fluxes(mass_per_volume, flow_speed, pressure, upstream_cotangent, eddy_viscosity):
    energy = pressure / (HEAT_RATIO - 1.0) + 0.5 * mass_per_volume * jnp.sum(
        flow_speed * flow_speed, 0
    )
    attenuation_coefficient = mass_per_volume * eddy_viscosity
    stagnation_specific_energy = energy + pressure
    directions = []
    for traversal_axis in range(3):
        transported_array = flow_speed[traversal_axis]
        partition_parts = [mass_per_volume * transported_array]
        for coordinate_slot in range(3):
            mass_flux_array = (
                mass_per_volume * flow_speed[coordinate_slot] * transported_array
                - attenuation_coefficient * upstream_cotangent[traversal_axis, coordinate_slot]
            )
            if coordinate_slot == traversal_axis:
                mass_flux_array = mass_flux_array + pressure
            partition_parts.append(mass_flux_array)
        partition_parts.append(
            stagnation_specific_energy * transported_array
            - THERMAL_DIFFUSE * attenuation_coefficient * upstream_cotangent[traversal_axis, 3]
        )
        directions.append(jnp.stack(partition_parts))
    return jnp.stack(directions)


def viscosity(upstream_cotangent, inner_weight, middle_weight, outer_weight):
    features = upstream_cotangent[:, :3].reshape((9,) + upstream_cotangent.shape[2:])
    hidden = jnp.tanh(
        jnp.einsum("hc,czxy->hzxy", inner_weight, features, precision=NETWORK_PRECISION)
    )
    hidden = jnp.tanh(
        jnp.einsum("hk,kzxy->hzxy", middle_weight, hidden, precision=NETWORK_PRECISION)
    )
    output = jnp.einsum("h,hzxy->zxy", outer_weight, hidden, precision=NETWORK_PRECISION)
    return EDDY_SCALE * jax.nn.softplus(output)


def local_flux(
    density_in, velocity_in, pressure_in, upstream_cotangent, inner_in, middle_in, outer_in
):
    eddy_viscosity = viscosity(upstream_cotangent, inner_in, middle_in, outer_in)
    return fluxes(density_in, velocity_in, pressure_in, upstream_cotangent, eddy_viscosity)


def compact_tables(x_cells, line_length):
    eye = np.eye(line_length)
    system = eye + COMPACT_ALPHA * (np.roll(eye, 1, 1) + np.roll(eye, -1, 1))
    right = np.zeros((line_length, line_length))
    cells = np.arange(line_length)
    for offset, value in (
        (1, 0.5 * COMPACT_NEAR),
        (-1, -0.5 * COMPACT_NEAR),
        (2, 0.25 * COMPACT_FAR),
        (-2, -0.25 * COMPACT_FAR),
    ):
        right[cells, (cells + offset) % line_length] += value
    row = np.linalg.solve(system, right)[0]

    def coef(offset):
        return row[offset % line_length]

    ratio = (-1.0 + np.sqrt(1.0 - 4.0 * COMPACT_ALPHA**2)) / (2.0 * COMPACT_ALPHA)
    gain = coef(NEAR_HALO + 1) / ratio ** (NEAR_HALO + 1)
    n, h = x_cells, NEAR_HALO
    own = np.arange(n)
    send = np.zeros((2 * h + 4, n))
    for k in range(h):
        send[k, n - h + k] = 1.0
    send[h, : n - h] = ratio ** (n - own[: n - h])
    send[h + 1] = ratio ** (2 * n - own)
    for k in range(h):
        send[h + 2 + k, k] = 1.0
    send[2 * h + 2, h:] = ratio ** own[h:]
    send[2 * h + 3] = ratio ** (n + own)
    width = n + 2 * h + 4
    take = np.zeros((n, width))
    for i in range(n):
        take[i, 0] = -gain * ratio**i
        for k in range(h):
            take[i, 1 + k] = coef(-h + k - i)
        take[i, 1 + h] = -gain * ratio**i
        for m in range(n):
            take[i, 2 + h + m] = coef(m - i)
        for k in range(h):
            take[i, 2 + h + n + k] = coef(n + k - i)
        take[i, 2 + 2 * h + n] = gain * ratio ** (n - i)
        take[i, 3 + 2 * h + n] = gain * ratio ** (n - i)
    return send, take


def x_send(fields):
    x_cells = fields.shape[2]
    h = NEAR_HALO
    send, _ = compact_tables(x_cells, x_cells * lax.axis_size("gx"))
    send = jnp.asarray(send, jnp.float32)
    planes = jnp.einsum("pj,fzjy->fzpy", send, fields, precision=HIGHEST_PRECISION)
    return (
        planes[:, :, : h + 1],
        planes[:, :, h + 1 : h + 2],
        planes[:, :, h + 2 : 2 * h + 3],
        planes[:, :, 2 * h + 3 :],
    )


def x_exchange(sent):
    to_right, to_right2, to_left, to_left2 = sent
    return (
        from_behind(to_right2, "gx", 2),
        from_behind(to_right, "gx", 1),
        from_behind(to_left, "gx", -1),
        from_behind(to_left2, "gx", -2),
    )


def x_finish(fields, sent, exchange=x_exchange):
    x_cells = fields.shape[2]
    h = NEAR_HALO
    _, take = compact_tables(x_cells, x_cells * lax.axis_size("gx"))
    take = jnp.asarray(take, jnp.float32)
    received = jnp.concatenate(exchange(sent), axis=2)
    take_own = take[:, h + 2 : h + 2 + x_cells]
    take_received = jnp.concatenate([take[:, : h + 2], take[:, h + 2 + x_cells :]], axis=1)
    own_part = jnp.einsum("ij,fzjy->fziy", take_own, fields, precision=HIGHEST_PRECISION)
    return own_part + jnp.einsum(
        "ij,fzjy->fziy", take_received, received, precision=HIGHEST_PRECISION
    )


def derive_x(fields):
    return x_finish(fields, x_send(fields))


def edge_send(block, axis, dim, width):
    size = block.shape[dim]
    low_part = lax.slice_in_dim(block, size - width, size, axis=dim)
    high_part = lax.slice_in_dim(block, 0, width, axis=dim)
    if lax.axis_size(axis) == 2:
        return (jnp.concatenate([low_part, high_part], axis=dim),)
    return (low_part, high_part)


def edge_exchange(sent, axis):
    if len(sent) == 1:
        return (from_behind(sent[0], axis, 1),)
    return (from_behind(sent[0], axis, 1), from_behind(sent[1], axis, -1))


def edge_combine(block, received, dim, width):
    if len(received) == 1:
        low = lax.slice_in_dim(received[0], 0, width, axis=dim)
        high = lax.slice_in_dim(received[0], width, 2 * width, axis=dim)
    else:
        low, high = received
    return jnp.concatenate([low, block, high], axis=dim)


def edge_finish(block, sent, axis, dim, width):
    return edge_combine(block, edge_exchange(sent, axis), dim, width)


def halo(block, axis, dim, width):
    return edge_finish(block, edge_send(block, axis, dim, width), axis, dim, width)


def centered(extended, along_axis, margin, length):

    def shifted(offset):
        return lax.slice_in_dim(
            extended, margin + offset, margin + offset + length, axis=along_axis
        )

    return (
        45.0 * (shifted(1) - shifted(-1))
        - 9.0 * (shifted(2) - shifted(-2))
        + (shifted(3) - shifted(-3))
    ) / 60.0


def derive_y(fields):
    return centered(halo(fields, "gy", 3, 3), 3, 3, fields.shape[3])


def derive_z(fields):
    return centered(halo(fields, "gz", 1, 3), 1, 3, fields.shape[1])


def butterfly_steps():
    steps = []
    for axis in ("gz", "gy", "gx"):
        count = lax.axis_size(axis)
        step = 1
        while step < count:
            steps.append((axis, step))
            step *= 2
    return steps


def butterfly_step(value, axis, step):
    count = lax.axis_size(axis)
    pairs = [(s, s ^ step) for s in range(count)]
    return value + lax.ppermute(value, axis, pairs)


def local(
    mass_per_volume, flow_speed, pressure, cotangent, weight_inner, weight_middle, weight_outer
):
    (state_now, scalars), prepare_pullback = jax.vjp(prepare, mass_per_volume, flow_speed, pressure)
    count = scalars.shape[0]
    first = jnp.concatenate([scalars, cotangent], 0)
    first_x = derive_x(first)
    first_y = derive_y(first)
    first_z = derive_z(first)
    gradients = jnp.stack([first_x[:count], first_y[:count], first_z[:count]])
    spread = jnp.stack([first_x[count:], first_y[count:], first_z[count:]])
    flux_all, flux_pullback = jax.vjp(
        local_flux,
        mass_per_volume,
        flow_speed,
        pressure,
        gradients,
        weight_inner,
        weight_middle,
        weight_outer,
    )
    pulled = flux_pullback(TIME_STEP * spread)
    gradient_bar = pulled[3]
    along_x = jnp.concatenate([flux_all[0], gradient_bar[0]], 0)
    along_y = jnp.concatenate([flux_all[1], gradient_bar[1]], 0)
    along_z = jnp.concatenate([flux_all[2], gradient_bar[2]], 0)
    weights = (pulled[4], pulled[5], pulled[6])
    flat = jnp.concatenate([w.reshape(-1) for w in weights])
    sent_x = x_send(along_x)
    sent_y = edge_send(along_y, "gy", 3, 3)
    sent_z = edge_send(along_z, "gz", 1, 3)
    sent_x, sent_y, sent_z, flat = lax.optimization_barrier((sent_x, sent_y, sent_z, flat))
    got_x = x_exchange(sent_x)
    got_y = edge_exchange(sent_y, "gy")
    got_z = edge_exchange(sent_z, "gz")
    steps = butterfly_steps()
    early = len(steps) - LATE_SUM_STEPS
    for axis, step in steps[:early]:
        flat = butterfly_step(flat, axis, step)
    got_x, got_y, got_z, flat = lax.optimization_barrier((got_x, got_y, got_z, flat))
    for axis, step in steps[early:]:
        flat = butterfly_step(flat, axis, step)
    second_x = x_finish(along_x, got_x, exchange=lambda received: received)
    second_y = centered(edge_combine(along_y, got_y, 3, 3), 3, 3, along_y.shape[3])
    second_z = centered(edge_combine(along_z, got_z, 1, 3), 1, 3, along_z.shape[1])
    second = second_x + second_y + second_z
    states = state_now.shape[0]
    state_next = state_now - TIME_STEP * second[:states]
    scalar_bar = -second[states:]
    direct = prepare_pullback((cotangent, scalar_bar))
    cells_all = (
        mass_per_volume.size * lax.axis_size("gx") * lax.axis_size("gy") * lax.axis_size("gz")
    )
    factor = 1.0 / math.sqrt(cells_all)
    totals = []
    start = 0
    for w in weights:
        totals.append(flat[start : start + w.size].reshape(w.shape) * factor)
        start += w.size
    return (
        state_next,
        direct[0] + pulled[0],
        direct[1] + pulled[1],
        direct[2] + pulled[2],
        totals[0],
        totals[1],
        totals[2],
    )


def solution(mesh):
    placed = (
        P("gz", "gx", "gy"),
        P(None, "gz", "gx", "gy"),
        P("gz", "gx", "gy"),
        P(None, "gz", "gx", "gy"),
        P(),
        P(),
        P(),
    )
    return jax.shard_map(
        local,
        mesh=mesh,
        in_specs=placed,
        out_specs=(
            P(None, "gz", "gx", "gy"),
            P("gz", "gx", "gy"),
            P(None, "gz", "gx", "gy"),
            P("gz", "gx", "gy"),
            P(),
            P(),
            P(),
        ),
        check_vma=False,
    )
```

```python
import math

import jax
import jax.numpy as jnp
import numpy as np
from jax import lax
from jax.sharding import PartitionSpec as P

HEAT_RATIO = 1.4
THERMAL_DIFFUSE = 3.5
EDDY_SCALE = 0.5
TIME_STEP = 0.1
COMPACT_ALPHA = 1.0 / 3.0
COMPACT_NEAR = 14.0 / 9.0
COMPACT_FAR = 1.0 / 9.0
HIGHEST_PRECISION = lax.Precision.HIGHEST
NEAR_HALO = 2
NETWORK_PRECISION = lax.Precision.HIGH


def from_behind(value, axis, steps):
    count = lax.axis_size(axis)
    pairs = [(source, (source + steps) % count) for source in range(count)]
    return lax.ppermute(value, axis, pairs)


def prepare(mass_per_volume, flow_speed, pressure):
    energy = pressure / (HEAT_RATIO - 1.0) + 0.5 * mass_per_volume * jnp.sum(
        flow_speed * flow_speed, 0
    )
    state_now = jnp.concatenate(
        [mass_per_volume[None], mass_per_volume[None] * flow_speed, energy[None]], 0
    )
    scalars = jnp.concatenate([flow_speed, (pressure / mass_per_volume)[None]], 0)
    return (state_now, scalars)


def fluxes(mass_per_volume, flow_speed, pressure, upstream_cotangent, eddy_viscosity):
    energy = pressure / (HEAT_RATIO - 1.0) + 0.5 * mass_per_volume * jnp.sum(
        flow_speed * flow_speed, 0
    )
    attenuation_coefficient = mass_per_volume * eddy_viscosity
    stagnation_specific_energy = energy + pressure
    directions = []
    for traversal_axis in range(3):
        transported_array = flow_speed[traversal_axis]
        partition_parts = [mass_per_volume * transported_array]
        for coordinate_slot in range(3):
            mass_flux_array = (
                mass_per_volume * flow_speed[coordinate_slot] * transported_array
                - attenuation_coefficient * upstream_cotangent[traversal_axis, coordinate_slot]
            )
            if coordinate_slot == traversal_axis:
                mass_flux_array = mass_flux_array + pressure
            partition_parts.append(mass_flux_array)
        partition_parts.append(
            stagnation_specific_energy * transported_array
            - THERMAL_DIFFUSE * attenuation_coefficient * upstream_cotangent[traversal_axis, 3]
        )
        directions.append(jnp.stack(partition_parts))
    return jnp.stack(directions)


def viscosity(upstream_cotangent, inner_weight, middle_weight, outer_weight):
    cells = upstream_cotangent.shape[2:]
    features = upstream_cotangent[:, :3].reshape((9, -1))
    hidden = jnp.tanh(jnp.dot(inner_weight, features, precision=NETWORK_PRECISION))
    hidden = jnp.tanh(jnp.dot(middle_weight, hidden, precision=NETWORK_PRECISION))
    output = jnp.dot(outer_weight, hidden, precision=NETWORK_PRECISION)
    return EDDY_SCALE * jax.nn.softplus(output).reshape(cells)


def local_flux(
    density_in, velocity_in, pressure_in, upstream_cotangent, inner_in, middle_in, outer_in
):
    eddy_viscosity = viscosity(upstream_cotangent, inner_in, middle_in, outer_in)
    return fluxes(density_in, velocity_in, pressure_in, upstream_cotangent, eddy_viscosity)


def compact_tables(x_cells, line_length):
    eye = np.eye(line_length)
    system = eye + COMPACT_ALPHA * (np.roll(eye, 1, 1) + np.roll(eye, -1, 1))
    right = np.zeros((line_length, line_length))
    cells = np.arange(line_length)
    for offset, value in (
        (1, 0.5 * COMPACT_NEAR),
        (-1, -0.5 * COMPACT_NEAR),
        (2, 0.25 * COMPACT_FAR),
        (-2, -0.25 * COMPACT_FAR),
    ):
        right[cells, (cells + offset) % line_length] += value
    row = np.linalg.solve(system, right)[0]

    def coef(offset):
        return row[offset % line_length]

    ratio = (-1.0 + np.sqrt(1.0 - 4.0 * COMPACT_ALPHA**2)) / (2.0 * COMPACT_ALPHA)
    gain = coef(NEAR_HALO + 1) / ratio ** (NEAR_HALO + 1)
    n, h = x_cells, NEAR_HALO
    own = np.arange(n)
    send = np.zeros((2 * h + 4, n))
    for k in range(h):
        send[k, n - h + k] = 1.0
    send[h, : n - h] = ratio ** (n - own[: n - h])
    send[h + 1] = ratio ** (2 * n - own)
    for k in range(h):
        send[h + 2 + k, k] = 1.0
    send[2 * h + 2, h:] = ratio ** own[h:]
    send[2 * h + 3] = ratio ** (n + own)
    width = n + 2 * h + 4
    take = np.zeros((n, width))
    for i in range(n):
        take[i, 0] = -gain * ratio**i
        for k in range(h):
            take[i, 1 + k] = coef(-h + k - i)
        take[i, 1 + h] = -gain * ratio**i
        for m in range(n):
            take[i, 2 + h + m] = coef(m - i)
        for k in range(h):
            take[i, 2 + h + n + k] = coef(n + k - i)
        take[i, 2 + 2 * h + n] = gain * ratio ** (n - i)
        take[i, 3 + 2 * h + n] = gain * ratio ** (n - i)
    return send, take


def derive_x(fields):
    x_cells = fields.shape[2]
    groups = lax.axis_size("gx")
    h = NEAR_HALO
    send, take = compact_tables(x_cells, x_cells * groups)
    send = jnp.asarray(send, jnp.float32)
    take = jnp.asarray(take, jnp.float32)
    planes = jnp.einsum("pj,fzjy->fzpy", send, fields, precision=HIGHEST_PRECISION)
    to_right = planes[:, :, : h + 1]
    to_right2 = planes[:, :, h + 1 : h + 2]
    to_left = planes[:, :, h + 2 : 2 * h + 3]
    to_left2 = planes[:, :, 2 * h + 3 :]
    from_left = from_behind(to_right, "gx", 1)
    from_left2 = from_behind(to_right2, "gx", 2)
    from_right = from_behind(to_left, "gx", -1)
    from_right2 = from_behind(to_left2, "gx", -2)
    received = jnp.concatenate([from_left2, from_left, from_right, from_right2], axis=2)
    take_own = take[:, h + 2 : h + 2 + x_cells]
    take_received = jnp.concatenate([take[:, : h + 2], take[:, h + 2 + x_cells :]], axis=1)
    own_part = jnp.einsum("ij,fzjy->fziy", take_own, fields, precision=HIGHEST_PRECISION)
    return own_part + jnp.einsum(
        "ij,fzjy->fziy", take_received, received, precision=HIGHEST_PRECISION
    )


def halo(block, axis, dim, width):
    count = lax.axis_size(axis)
    size = block.shape[dim]
    low_part = lax.slice_in_dim(block, size - width, size, axis=dim)
    high_part = lax.slice_in_dim(block, 0, width, axis=dim)
    if count == 2:
        both = from_behind(jnp.concatenate([low_part, high_part], axis=dim), axis, 1)
        low = lax.slice_in_dim(both, 0, width, axis=dim)
        high = lax.slice_in_dim(both, width, 2 * width, axis=dim)
    else:
        low = from_behind(low_part, axis, 1)
        high = from_behind(high_part, axis, -1)
    return jnp.concatenate([low, block, high], axis=dim)


def centered(extended, along_axis, margin, length):

    def shifted(offset):
        return lax.slice_in_dim(
            extended, margin + offset, margin + offset + length, axis=along_axis
        )

    return (
        45.0 * (shifted(1) - shifted(-1))
        - 9.0 * (shifted(2) - shifted(-2))
        + (shifted(3) - shifted(-3))
    ) / 60.0


def derive_y(fields):
    return centered(halo(fields, "gy", 3, 3), 3, 3, fields.shape[3])


def derive_z(fields):
    return centered(halo(fields, "gz", 1, 3), 1, 3, fields.shape[1])


def butterfly_sum(value, axis):
    count = lax.axis_size(axis)
    step = 1
    while step < count:
        if count % (2 * step) == 0:
            pairs = [(s, s ^ step) for s in range(count)]
            value = value + lax.ppermute(value, axis, pairs)
            step *= 2
        else:
            return lax.psum(value, axis)
    return value


def local(
    mass_per_volume, flow_speed, pressure, cotangent, weight_inner, weight_middle, weight_outer
):
    (state_now, scalars), prepare_pullback = jax.vjp(prepare, mass_per_volume, flow_speed, pressure)
    count = scalars.shape[0]
    first = jnp.concatenate([scalars, cotangent], 0)
    first_x = derive_x(first)
    first_y = derive_y(first)
    first_z = derive_z(first)
    gradients = jnp.stack([first_x[:count], first_y[:count], first_z[:count]])
    spread = jnp.stack([first_x[count:], first_y[count:], first_z[count:]])
    flux_all, flux_pullback = jax.vjp(
        local_flux,
        mass_per_volume,
        flow_speed,
        pressure,
        gradients,
        weight_inner,
        weight_middle,
        weight_outer,
    )
    pulled = flux_pullback(TIME_STEP * spread)
    gradient_bar = pulled[3]
    second_x = derive_x(jnp.concatenate([flux_all[0], gradient_bar[0]], 0))
    second_y = derive_y(jnp.concatenate([flux_all[1], gradient_bar[1]], 0))
    second_z = derive_z(jnp.concatenate([flux_all[2], gradient_bar[2]], 0))
    second = second_x + second_y + second_z
    states = state_now.shape[0]
    state_next = state_now - TIME_STEP * second[:states]
    scalar_bar = -second[states:]
    direct = prepare_pullback((cotangent, scalar_bar))
    weights = (pulled[4], pulled[5], pulled[6])
    flat = jnp.concatenate([w.reshape(-1) for w in weights])
    for axis in ("gz", "gy", "gx"):
        flat = butterfly_sum(flat, axis)
    cells_all = (
        mass_per_volume.size * lax.axis_size("gx") * lax.axis_size("gy") * lax.axis_size("gz")
    )
    factor = 1.0 / math.sqrt(cells_all)
    totals = []
    start = 0
    for w in weights:
        totals.append(flat[start : start + w.size].reshape(w.shape) * factor)
        start += w.size
    return (
        state_next,
        direct[0] + pulled[0],
        direct[1] + pulled[1],
        direct[2] + pulled[2],
        totals[0],
        totals[1],
        totals[2],
    )


def solution(mesh):
    placed = (
        P("gz", "gx", "gy"),
        P(None, "gz", "gx", "gy"),
        P("gz", "gx", "gy"),
        P(None, "gz", "gx", "gy"),
        P(),
        P(),
        P(),
    )
    return jax.shard_map(
        local,
        mesh=mesh,
        in_specs=placed,
        out_specs=(
            P(None, "gz", "gx", "gy"),
            P("gz", "gx", "gy"),
            P(None, "gz", "gx", "gy"),
            P("gz", "gx", "gy"),
            P(),
            P(),
            P(),
        ),
        check_vma=False,
    )
```

```python
import math

import jax
import jax.numpy as jnp
import numpy as np
from jax import lax
from jax.experimental import pallas as pl
from jax.experimental.pallas import tpu as pltpu
from jax.sharding import PartitionSpec as P

HEAT_RATIO = 1.4
THERMAL_DIFFUSE = 3.5
EDDY_SCALE = 0.5
TIME_STEP = 0.1
COMPACT_ALPHA = 1.0 / 3.0
COMPACT_NEAR = 14.0 / 9.0
COMPACT_FAR = 1.0 / 9.0
HIGHEST_PRECISION = lax.Precision.HIGHEST
NEAR_HALO = 2
NETWORK_PRECISION = lax.Precision.HIGH
NETWORK_BLOCK = 2048


def from_behind(value, axis, steps):
    count = lax.axis_size(axis)
    pairs = [(source, (source + steps) % count) for source in range(count)]
    return lax.ppermute(value, axis, pairs)


def prepare(mass_per_volume, flow_speed, pressure):
    energy = pressure / (HEAT_RATIO - 1.0) + 0.5 * mass_per_volume * jnp.sum(
        flow_speed * flow_speed, 0
    )
    state_now = jnp.concatenate(
        [mass_per_volume[None], mass_per_volume[None] * flow_speed, energy[None]], 0
    )
    scalars = jnp.concatenate([flow_speed, (pressure / mass_per_volume)[None]], 0)
    return (state_now, scalars)


def fluxes(mass_per_volume, flow_speed, pressure, upstream_cotangent, eddy_viscosity):
    energy = pressure / (HEAT_RATIO - 1.0) + 0.5 * mass_per_volume * jnp.sum(
        flow_speed * flow_speed, 0
    )
    attenuation_coefficient = mass_per_volume * eddy_viscosity
    stagnation_specific_energy = energy + pressure
    directions = []
    for traversal_axis in range(3):
        transported_array = flow_speed[traversal_axis]
        partition_parts = [mass_per_volume * transported_array]
        for coordinate_slot in range(3):
            mass_flux_array = (
                mass_per_volume * flow_speed[coordinate_slot] * transported_array
                - attenuation_coefficient * upstream_cotangent[traversal_axis, coordinate_slot]
            )
            if coordinate_slot == traversal_axis:
                mass_flux_array = mass_flux_array + pressure
            partition_parts.append(mass_flux_array)
        partition_parts.append(
            stagnation_specific_energy * transported_array
            - THERMAL_DIFFUSE * attenuation_coefficient * upstream_cotangent[traversal_axis, 3]
        )
        directions.append(jnp.stack(partition_parts))
    return jnp.stack(directions)


def viscosity(upstream_cotangent, inner_weight, middle_weight, outer_weight):
    features = upstream_cotangent[:, :3].reshape((9,) + upstream_cotangent.shape[2:])
    hidden = jnp.tanh(
        jnp.einsum("hc,czxy->hzxy", inner_weight, features, precision=NETWORK_PRECISION)
    )
    hidden = jnp.tanh(
        jnp.einsum("hk,kzxy->hzxy", middle_weight, hidden, precision=NETWORK_PRECISION)
    )
    output = jnp.einsum("h,hzxy->zxy", outer_weight, hidden, precision=NETWORK_PRECISION)
    return EDDY_SCALE * jax.nn.softplus(output)


def local_flux(
    density_in, velocity_in, pressure_in, upstream_cotangent, inner_in, middle_in, outer_in
):
    eddy_viscosity = viscosity(upstream_cotangent, inner_in, middle_in, outer_in)
    return fluxes(density_in, velocity_in, pressure_in, upstream_cotangent, eddy_viscosity)


def network_kernel(
    features_ref, eddy_bar_ref, inner_ref, inner_t_ref, middle_ref, middle_t_ref, outer_ref,
    eddy_ref, features_bar_ref, inner_bar_ref, middle_bar_ref, outer_bar_ref,
):
    exact = lax.Precision.HIGHEST
    features = features_ref[...]
    first = jnp.tanh(jnp.dot(inner_ref[...], features, precision=exact))
    second = jnp.tanh(jnp.dot(middle_ref[...], first, precision=exact))
    output = jnp.sum(outer_ref[...] * second, axis=0, keepdims=True)
    soft = jnp.maximum(output, 0.0) + jnp.log1p(jnp.exp(-jnp.abs(output)))
    eddy_ref[...] = EDDY_SCALE * soft
    output_bar = EDDY_SCALE * eddy_bar_ref[...] / (1.0 + jnp.exp(-output))
    second_pre_bar = outer_ref[...] * output_bar * (1.0 - second * second)
    first_pre_bar = jnp.dot(middle_t_ref[...], second_pre_bar, precision=exact) * (
        1.0 - first * first
    )
    features_bar_ref[...] = jnp.dot(inner_t_ref[...], first_pre_bar, precision=exact)
    by_cells = (((1,), (1,)), ((), ()))
    middle_part = lax.dot_general(second_pre_bar, first, by_cells, precision=exact)
    inner_part = lax.dot_general(first_pre_bar, features, by_cells, precision=exact)
    outer_part = jnp.sum(second * output_bar, axis=1, keepdims=True)

    @pl.when(pl.program_id(0) == 0)
    def _():
        inner_bar_ref[...] = jnp.zeros_like(inner_bar_ref)
        middle_bar_ref[...] = jnp.zeros_like(middle_bar_ref)
        outer_bar_ref[...] = jnp.zeros_like(outer_bar_ref)

    inner_bar_ref[...] += inner_part
    middle_bar_ref[...] += middle_part
    outer_bar_ref[...] += outer_part


def network(features, eddy_bar, inner_weight, middle_weight, outer_weight):
    inputs, cells = features.shape
    hidden = inner_weight.shape[0]
    block = min(NETWORK_BLOCK, cells)
    outer_column = outer_weight.reshape(hidden, 1)

    def whole(shape):
        return pl.BlockSpec(shape, lambda i: (0, 0))

    def lanes(rows):
        return pl.BlockSpec((rows, block), lambda i: (0, i))

    return pl.pallas_call(
        network_kernel,
        grid=(cells // block,),
        in_specs=[
            lanes(inputs),
            lanes(1),
            whole((hidden, inputs)),
            whole((inputs, hidden)),
            whole((hidden, hidden)),
            whole((hidden, hidden)),
            whole((hidden, 1)),
        ],
        out_specs=[
            lanes(1),
            lanes(inputs),
            whole((hidden, inputs)),
            whole((hidden, hidden)),
            whole((hidden, 1)),
        ],
        out_shape=[
            jax.ShapeDtypeStruct((1, cells), jnp.float32),
            jax.ShapeDtypeStruct((inputs, cells), jnp.float32),
            jax.ShapeDtypeStruct((hidden, inputs), jnp.float32),
            jax.ShapeDtypeStruct((hidden, hidden), jnp.float32),
            jax.ShapeDtypeStruct((hidden, 1), jnp.float32),
        ],
        compiler_params=pltpu.CompilerParams(dimension_semantics=("arbitrary",)),
    )(features, eddy_bar, inner_weight, inner_weight.T, middle_weight, middle_weight.T, outer_column)


def compact_tables(x_cells, line_length):
    eye = np.eye(line_length)
    system = eye + COMPACT_ALPHA * (np.roll(eye, 1, 1) + np.roll(eye, -1, 1))
    right = np.zeros((line_length, line_length))
    cells = np.arange(line_length)
    for offset, value in (
        (1, 0.5 * COMPACT_NEAR),
        (-1, -0.5 * COMPACT_NEAR),
        (2, 0.25 * COMPACT_FAR),
        (-2, -0.25 * COMPACT_FAR),
    ):
        right[cells, (cells + offset) % line_length] += value
    row = np.linalg.solve(system, right)[0]

    def coef(offset):
        return row[offset % line_length]

    ratio = (-1.0 + np.sqrt(1.0 - 4.0 * COMPACT_ALPHA**2)) / (2.0 * COMPACT_ALPHA)
    gain = coef(NEAR_HALO + 1) / ratio ** (NEAR_HALO + 1)
    n, h = x_cells, NEAR_HALO
    own = np.arange(n)
    send = np.zeros((2 * h + 4, n))
    for k in range(h):
        send[k, n - h + k] = 1.0
    send[h, : n - h] = ratio ** (n - own[: n - h])
    send[h + 1] = ratio ** (2 * n - own)
    for k in range(h):
        send[h + 2 + k, k] = 1.0
    send[2 * h + 2, h:] = ratio ** own[h:]
    send[2 * h + 3] = ratio ** (n + own)
    width = n + 2 * h + 4
    take = np.zeros((n, width))
    for i in range(n):
        take[i, 0] = -gain * ratio**i
        for k in range(h):
            take[i, 1 + k] = coef(-h + k - i)
        take[i, 1 + h] = -gain * ratio**i
        for m in range(n):
            take[i, 2 + h + m] = coef(m - i)
        for k in range(h):
            take[i, 2 + h + n + k] = coef(n + k - i)
        take[i, 2 + 2 * h + n] = gain * ratio ** (n - i)
        take[i, 3 + 2 * h + n] = gain * ratio ** (n - i)
    return send, take


def derive_x(fields):
    x_cells = fields.shape[2]
    groups = lax.axis_size("gx")
    h = NEAR_HALO
    send, take = compact_tables(x_cells, x_cells * groups)
    send = jnp.asarray(send, jnp.float32)
    take = jnp.asarray(take, jnp.float32)
    planes = jnp.einsum("pj,fzjy->fzpy", send, fields, precision=HIGHEST_PRECISION)
    to_right = planes[:, :, : h + 1]
    to_right2 = planes[:, :, h + 1 : h + 2]
    to_left = planes[:, :, h + 2 : 2 * h + 3]
    to_left2 = planes[:, :, 2 * h + 3 :]
    from_left = from_behind(to_right, "gx", 1)
    from_left2 = from_behind(to_right2, "gx", 2)
    from_right = from_behind(to_left, "gx", -1)
    from_right2 = from_behind(to_left2, "gx", -2)
    received = jnp.concatenate([from_left2, from_left, from_right, from_right2], axis=2)
    take_own = take[:, h + 2 : h + 2 + x_cells]
    take_received = jnp.concatenate([take[:, : h + 2], take[:, h + 2 + x_cells :]], axis=1)
    own_part = jnp.einsum("ij,fzjy->fziy", take_own, fields, precision=HIGHEST_PRECISION)
    return own_part + jnp.einsum(
        "ij,fzjy->fziy", take_received, received, precision=HIGHEST_PRECISION
    )


def halo(block, axis, dim, width):
    count = lax.axis_size(axis)
    size = block.shape[dim]
    low_part = lax.slice_in_dim(block, size - width, size, axis=dim)
    high_part = lax.slice_in_dim(block, 0, width, axis=dim)
    if count == 2:
        both = from_behind(jnp.concatenate([low_part, high_part], axis=dim), axis, 1)
        low = lax.slice_in_dim(both, 0, width, axis=dim)
        high = lax.slice_in_dim(both, width, 2 * width, axis=dim)
    else:
        low = from_behind(low_part, axis, 1)
        high = from_behind(high_part, axis, -1)
    return jnp.concatenate([low, block, high], axis=dim)


def centered(extended, along_axis, margin, length):

    def shifted(offset):
        return lax.slice_in_dim(
            extended, margin + offset, margin + offset + length, axis=along_axis
        )

    return (
        45.0 * (shifted(1) - shifted(-1))
        - 9.0 * (shifted(2) - shifted(-2))
        + (shifted(3) - shifted(-3))
    ) / 60.0


def derive_y(fields):
    return centered(halo(fields, "gy", 3, 3), 3, 3, fields.shape[3])


def derive_z(fields):
    return centered(halo(fields, "gz", 1, 3), 1, 3, fields.shape[1])


def butterfly_sum(value, axis):
    count = lax.axis_size(axis)
    step = 1
    while step < count:
        if count % (2 * step) == 0:
            pairs = [(s, s ^ step) for s in range(count)]
            value = value + lax.ppermute(value, axis, pairs)
            step *= 2
        else:
            return lax.psum(value, axis)
    return value


def local(
    mass_per_volume, flow_speed, pressure, cotangent, weight_inner, weight_middle, weight_outer
):
    (state_now, scalars), prepare_pullback = jax.vjp(prepare, mass_per_volume, flow_speed, pressure)
    count = scalars.shape[0]
    first = jnp.concatenate([scalars, cotangent], 0)
    first_x = derive_x(first)
    first_y = derive_y(first)
    first_z = derive_z(first)
    gradients = jnp.stack([first_x[:count], first_y[:count], first_z[:count]])
    spread = jnp.stack([first_x[count:], first_y[count:], first_z[count:]])
    flux_bar = TIME_STEP * spread
    cells = mass_per_volume.shape

    def flux_of(eddy_viscosity):
        return fluxes(mass_per_volume, flow_speed, pressure, gradients, eddy_viscosity)

    _, eddy_pullback = jax.vjp(flux_of, jnp.zeros(cells, jnp.float32))
    (eddy_bar,) = eddy_pullback(flux_bar)
    features = gradients[:, :3].reshape((9, -1))
    eddy, features_bar, inner_bar, middle_bar, outer_bar = network(
        features, eddy_bar.reshape(1, -1), weight_inner, weight_middle, weight_outer
    )
    flux_all, flux_pullback = jax.vjp(
        fluxes, mass_per_volume, flow_speed, pressure, gradients, eddy.reshape(cells)
    )
    pulled = flux_pullback(flux_bar)
    features_bar = features_bar.reshape((3, 3) + cells)
    pulled = (
        pulled[0],
        pulled[1],
        pulled[2],
        pulled[3].at[:, :3].add(features_bar),
        inner_bar,
        middle_bar,
        outer_bar.reshape(-1),
    )
    gradient_bar = pulled[3]
    second_x = derive_x(jnp.concatenate([flux_all[0], gradient_bar[0]], 0))
    second_y = derive_y(jnp.concatenate([flux_all[1], gradient_bar[1]], 0))
    second_z = derive_z(jnp.concatenate([flux_all[2], gradient_bar[2]], 0))
    second = second_x + second_y + second_z
    states = state_now.shape[0]
    state_next = state_now - TIME_STEP * second[:states]
    scalar_bar = -second[states:]
    direct = prepare_pullback((cotangent, scalar_bar))
    weights = (pulled[4], pulled[5], pulled[6])
    flat = jnp.concatenate([w.reshape(-1) for w in weights])
    for axis in ("gz", "gy", "gx"):
        flat = butterfly_sum(flat, axis)
    cells_all = (
        mass_per_volume.size * lax.axis_size("gx") * lax.axis_size("gy") * lax.axis_size("gz")
    )
    factor = 1.0 / math.sqrt(cells_all)
    totals = []
    start = 0
    for w in weights:
        totals.append(flat[start : start + w.size].reshape(w.shape) * factor)
        start += w.size
    return (
        state_next,
        direct[0] + pulled[0],
        direct[1] + pulled[1],
        direct[2] + pulled[2],
        totals[0],
        totals[1],
        totals[2],
    )


def solution(mesh):
    placed = (
        P("gz", "gx", "gy"),
        P(None, "gz", "gx", "gy"),
        P("gz", "gx", "gy"),
        P(None, "gz", "gx", "gy"),
        P(),
        P(),
        P(),
    )
    return jax.shard_map(
        local,
        mesh=mesh,
        in_specs=placed,
        out_specs=(
            P(None, "gz", "gx", "gy"),
            P("gz", "gx", "gy"),
            P(None, "gz", "gx", "gy"),
            P("gz", "gx", "gy"),
            P(),
            P(),
            P(),
        ),
        check_vma=False,
    )
```

```python
import math

import jax
import jax.numpy as jnp
import numpy as np
from jax import lax
from jax.experimental import pallas as pl
from jax.experimental.pallas import tpu as pltpu
from jax.sharding import PartitionSpec as P

HEAT_RATIO = 1.4
THERMAL_DIFFUSE = 3.5
EDDY_SCALE = 0.5
TIME_STEP = 0.1
COMPACT_ALPHA = 1.0 / 3.0
COMPACT_NEAR = 14.0 / 9.0
COMPACT_FAR = 1.0 / 9.0
HIGHEST_PRECISION = lax.Precision.HIGHEST
NEAR_HALO = 2
NETWORK_PRECISION = lax.Precision.HIGH
NETWORK_BLOCK = 4096


def from_behind(value, axis, steps):
    count = lax.axis_size(axis)
    pairs = [(source, (source + steps) % count) for source in range(count)]
    return lax.ppermute(value, axis, pairs)


def prepare(mass_per_volume, flow_speed, pressure):
    energy = pressure / (HEAT_RATIO - 1.0) + 0.5 * mass_per_volume * jnp.sum(
        flow_speed * flow_speed, 0
    )
    state_now = jnp.concatenate(
        [mass_per_volume[None], mass_per_volume[None] * flow_speed, energy[None]], 0
    )
    scalars = jnp.concatenate([flow_speed, (pressure / mass_per_volume)[None]], 0)
    return (state_now, scalars)


def fluxes(mass_per_volume, flow_speed, pressure, upstream_cotangent, eddy_viscosity):
    energy = pressure / (HEAT_RATIO - 1.0) + 0.5 * mass_per_volume * jnp.sum(
        flow_speed * flow_speed, 0
    )
    attenuation_coefficient = mass_per_volume * eddy_viscosity
    stagnation_specific_energy = energy + pressure
    directions = []
    for traversal_axis in range(3):
        transported_array = flow_speed[traversal_axis]
        partition_parts = [mass_per_volume * transported_array]
        for coordinate_slot in range(3):
            mass_flux_array = (
                mass_per_volume * flow_speed[coordinate_slot] * transported_array
                - attenuation_coefficient * upstream_cotangent[traversal_axis, coordinate_slot]
            )
            if coordinate_slot == traversal_axis:
                mass_flux_array = mass_flux_array + pressure
            partition_parts.append(mass_flux_array)
        partition_parts.append(
            stagnation_specific_energy * transported_array
            - THERMAL_DIFFUSE * attenuation_coefficient * upstream_cotangent[traversal_axis, 3]
        )
        directions.append(jnp.stack(partition_parts))
    return jnp.stack(directions)


def viscosity(upstream_cotangent, inner_weight, middle_weight, outer_weight):
    features = upstream_cotangent[:, :3].reshape((9,) + upstream_cotangent.shape[2:])
    hidden = jnp.tanh(
        jnp.einsum("hc,czxy->hzxy", inner_weight, features, precision=NETWORK_PRECISION)
    )
    hidden = jnp.tanh(
        jnp.einsum("hk,kzxy->hzxy", middle_weight, hidden, precision=NETWORK_PRECISION)
    )
    output = jnp.einsum("h,hzxy->zxy", outer_weight, hidden, precision=NETWORK_PRECISION)
    return EDDY_SCALE * jax.nn.softplus(output)


def local_flux(
    density_in, velocity_in, pressure_in, upstream_cotangent, inner_in, middle_in, outer_in
):
    eddy_viscosity = viscosity(upstream_cotangent, inner_in, middle_in, outer_in)
    return fluxes(density_in, velocity_in, pressure_in, upstream_cotangent, eddy_viscosity)


def split_bf16(value):
    high = value.astype(jnp.bfloat16)
    low = (value - high.astype(jnp.float32)).astype(jnp.bfloat16)
    return high, low


def dot3(left, right, dims=(((1,), (0,)), ((), ()))):
    left_high, left_low = left
    right_high, right_low = right

    def one(a, b):
        return lax.dot_general(a, b, dims, preferred_element_type=jnp.float32)

    return one(left_high, right_high) + (one(left_high, right_low) + one(left_low, right_high))


def network_kernel(
    features_ref, eddy_bar_ref, inner_ref, inner_t_ref, middle_ref, middle_t_ref, outer_ref,
    eddy_ref, features_bar_ref, inner_bar_ref, middle_bar_ref, outer_bar_ref,
):
    features = split_bf16(features_ref[...])
    first = jnp.tanh(dot3(split_bf16(inner_ref[...]), features))
    first_split = split_bf16(first)
    second = jnp.tanh(dot3(split_bf16(middle_ref[...]), first_split))
    output = jnp.sum(outer_ref[...] * second, axis=0, keepdims=True)
    soft = jnp.maximum(output, 0.0) + jnp.log1p(jnp.exp(-jnp.abs(output)))
    eddy_ref[...] = EDDY_SCALE * soft
    output_bar = EDDY_SCALE * eddy_bar_ref[...] / (1.0 + jnp.exp(-output))
    second_pre_bar = split_bf16(outer_ref[...] * output_bar * (1.0 - second * second))
    first_pre_bar = dot3(split_bf16(middle_t_ref[...]), second_pre_bar) * (1.0 - first * first)
    first_pre_bar = split_bf16(first_pre_bar)
    features_bar_ref[...] = dot3(split_bf16(inner_t_ref[...]), first_pre_bar)
    by_cells = (((1,), (1,)), ((), ()))
    middle_part = dot3(second_pre_bar, first_split, by_cells)
    inner_part = dot3(first_pre_bar, features, by_cells)
    outer_part = jnp.sum(second * output_bar, axis=1, keepdims=True)

    @pl.when(pl.program_id(0) == 0)
    def _():
        inner_bar_ref[...] = jnp.zeros_like(inner_bar_ref)
        middle_bar_ref[...] = jnp.zeros_like(middle_bar_ref)
        outer_bar_ref[...] = jnp.zeros_like(outer_bar_ref)

    inner_bar_ref[...] += inner_part
    middle_bar_ref[...] += middle_part
    outer_bar_ref[...] += outer_part


def network(features, eddy_bar, inner_weight, middle_weight, outer_weight):
    inputs, cells = features.shape
    hidden = inner_weight.shape[0]
    block = min(NETWORK_BLOCK, cells)
    outer_column = outer_weight.reshape(hidden, 1)

    def whole(shape):
        return pl.BlockSpec(shape, lambda i: (0, 0))

    def lanes(rows):
        return pl.BlockSpec((rows, block), lambda i: (0, i))

    return pl.pallas_call(
        network_kernel,
        grid=(cells // block,),
        in_specs=[
            lanes(inputs),
            lanes(1),
            whole((hidden, inputs)),
            whole((inputs, hidden)),
            whole((hidden, hidden)),
            whole((hidden, hidden)),
            whole((hidden, 1)),
        ],
        out_specs=[
            lanes(1),
            lanes(inputs),
            whole((hidden, inputs)),
            whole((hidden, hidden)),
            whole((hidden, 1)),
        ],
        out_shape=[
            jax.ShapeDtypeStruct((1, cells), jnp.float32),
            jax.ShapeDtypeStruct((inputs, cells), jnp.float32),
            jax.ShapeDtypeStruct((hidden, inputs), jnp.float32),
            jax.ShapeDtypeStruct((hidden, hidden), jnp.float32),
            jax.ShapeDtypeStruct((hidden, 1), jnp.float32),
        ],
        compiler_params=pltpu.CompilerParams(dimension_semantics=("arbitrary",)),
    )(features, eddy_bar, inner_weight, inner_weight.T, middle_weight, middle_weight.T, outer_column)


def compact_tables(x_cells, line_length):
    eye = np.eye(line_length)
    system = eye + COMPACT_ALPHA * (np.roll(eye, 1, 1) + np.roll(eye, -1, 1))
    right = np.zeros((line_length, line_length))
    cells = np.arange(line_length)
    for offset, value in (
        (1, 0.5 * COMPACT_NEAR),
        (-1, -0.5 * COMPACT_NEAR),
        (2, 0.25 * COMPACT_FAR),
        (-2, -0.25 * COMPACT_FAR),
    ):
        right[cells, (cells + offset) % line_length] += value
    row = np.linalg.solve(system, right)[0]

    def coef(offset):
        return row[offset % line_length]

    ratio = (-1.0 + np.sqrt(1.0 - 4.0 * COMPACT_ALPHA**2)) / (2.0 * COMPACT_ALPHA)
    gain = coef(NEAR_HALO + 1) / ratio ** (NEAR_HALO + 1)
    n, h = x_cells, NEAR_HALO
    own = np.arange(n)
    send = np.zeros((2 * h + 4, n))
    for k in range(h):
        send[k, n - h + k] = 1.0
    send[h, : n - h] = ratio ** (n - own[: n - h])
    send[h + 1] = ratio ** (2 * n - own)
    for k in range(h):
        send[h + 2 + k, k] = 1.0
    send[2 * h + 2, h:] = ratio ** own[h:]
    send[2 * h + 3] = ratio ** (n + own)
    width = n + 2 * h + 4
    take = np.zeros((n, width))
    for i in range(n):
        take[i, 0] = -gain * ratio**i
        for k in range(h):
            take[i, 1 + k] = coef(-h + k - i)
        take[i, 1 + h] = -gain * ratio**i
        for m in range(n):
            take[i, 2 + h + m] = coef(m - i)
        for k in range(h):
            take[i, 2 + h + n + k] = coef(n + k - i)
        take[i, 2 + 2 * h + n] = gain * ratio ** (n - i)
        take[i, 3 + 2 * h + n] = gain * ratio ** (n - i)
    return send, take


def derive_x(fields):
    x_cells = fields.shape[2]
    groups = lax.axis_size("gx")
    h = NEAR_HALO
    send, take = compact_tables(x_cells, x_cells * groups)
    send = jnp.asarray(send, jnp.float32)
    take = jnp.asarray(take, jnp.float32)
    planes = jnp.einsum("pj,fzjy->fzpy", send, fields, precision=HIGHEST_PRECISION)
    to_right = planes[:, :, : h + 1]
    to_right2 = planes[:, :, h + 1 : h + 2]
    to_left = planes[:, :, h + 2 : 2 * h + 3]
    to_left2 = planes[:, :, 2 * h + 3 :]
    from_left = from_behind(to_right, "gx", 1)
    from_left2 = from_behind(to_right2, "gx", 2)
    from_right = from_behind(to_left, "gx", -1)
    from_right2 = from_behind(to_left2, "gx", -2)
    received = jnp.concatenate([from_left2, from_left, from_right, from_right2], axis=2)
    take_own = take[:, h + 2 : h + 2 + x_cells]
    take_received = jnp.concatenate([take[:, : h + 2], take[:, h + 2 + x_cells :]], axis=1)
    own_part = jnp.einsum("ij,fzjy->fziy", take_own, fields, precision=HIGHEST_PRECISION)
    return own_part + jnp.einsum(
        "ij,fzjy->fziy", take_received, received, precision=HIGHEST_PRECISION
    )


def halo(block, axis, dim, width):
    count = lax.axis_size(axis)
    size = block.shape[dim]
    low_part = lax.slice_in_dim(block, size - width, size, axis=dim)
    high_part = lax.slice_in_dim(block, 0, width, axis=dim)
    if count == 2:
        both = from_behind(jnp.concatenate([low_part, high_part], axis=dim), axis, 1)
        low = lax.slice_in_dim(both, 0, width, axis=dim)
        high = lax.slice_in_dim(both, width, 2 * width, axis=dim)
    else:
        low = from_behind(low_part, axis, 1)
        high = from_behind(high_part, axis, -1)
    return jnp.concatenate([low, block, high], axis=dim)


def centered(extended, along_axis, margin, length):

    def shifted(offset):
        return lax.slice_in_dim(
            extended, margin + offset, margin + offset + length, axis=along_axis
        )

    return (
        45.0 * (shifted(1) - shifted(-1))
        - 9.0 * (shifted(2) - shifted(-2))
        + (shifted(3) - shifted(-3))
    ) / 60.0


def derive_y(fields):
    return centered(halo(fields, "gy", 3, 3), 3, 3, fields.shape[3])


def derive_z(fields):
    return centered(halo(fields, "gz", 1, 3), 1, 3, fields.shape[1])


def butterfly_sum(value, axis):
    count = lax.axis_size(axis)
    step = 1
    while step < count:
        if count % (2 * step) == 0:
            pairs = [(s, s ^ step) for s in range(count)]
            value = value + lax.ppermute(value, axis, pairs)
            step *= 2
        else:
            return lax.psum(value, axis)
    return value


def local(
    mass_per_volume, flow_speed, pressure, cotangent, weight_inner, weight_middle, weight_outer
):
    (state_now, scalars), prepare_pullback = jax.vjp(prepare, mass_per_volume, flow_speed, pressure)
    count = scalars.shape[0]
    first = jnp.concatenate([scalars, cotangent], 0)
    first_x = derive_x(first)
    first_y = derive_y(first)
    first_z = derive_z(first)
    gradients = jnp.stack([first_x[:count], first_y[:count], first_z[:count]])
    spread = jnp.stack([first_x[count:], first_y[count:], first_z[count:]])
    flux_bar = TIME_STEP * spread
    cells = mass_per_volume.shape

    def flux_of(eddy_viscosity):
        return fluxes(mass_per_volume, flow_speed, pressure, gradients, eddy_viscosity)

    _, eddy_pullback = jax.vjp(flux_of, jnp.zeros(cells, jnp.float32))
    (eddy_bar,) = eddy_pullback(flux_bar)
    features = gradients[:, :3].reshape((9, -1))
    eddy, features_bar, inner_bar, middle_bar, outer_bar = network(
        features, eddy_bar.reshape(1, -1), weight_inner, weight_middle, weight_outer
    )
    flux_all, flux_pullback = jax.vjp(
        fluxes, mass_per_volume, flow_speed, pressure, gradients, eddy.reshape(cells)
    )
    pulled = flux_pullback(flux_bar)
    features_bar = features_bar.reshape((3, 3) + cells)
    pulled = (
        pulled[0],
        pulled[1],
        pulled[2],
        pulled[3].at[:, :3].add(features_bar),
        inner_bar,
        middle_bar,
        outer_bar.reshape(-1),
    )
    gradient_bar = pulled[3]
    second_x = derive_x(jnp.concatenate([flux_all[0], gradient_bar[0]], 0))
    second_y = derive_y(jnp.concatenate([flux_all[1], gradient_bar[1]], 0))
    second_z = derive_z(jnp.concatenate([flux_all[2], gradient_bar[2]], 0))
    second = second_x + second_y + second_z
    states = state_now.shape[0]
    state_next = state_now - TIME_STEP * second[:states]
    scalar_bar = -second[states:]
    direct = prepare_pullback((cotangent, scalar_bar))
    weights = (pulled[4], pulled[5], pulled[6])
    flat = jnp.concatenate([w.reshape(-1) for w in weights])
    for axis in ("gz", "gy", "gx"):
        flat = butterfly_sum(flat, axis)
    cells_all = (
        mass_per_volume.size * lax.axis_size("gx") * lax.axis_size("gy") * lax.axis_size("gz")
    )
    factor = 1.0 / math.sqrt(cells_all)
    totals = []
    start = 0
    for w in weights:
        totals.append(flat[start : start + w.size].reshape(w.shape) * factor)
        start += w.size
    return (
        state_next,
        direct[0] + pulled[0],
        direct[1] + pulled[1],
        direct[2] + pulled[2],
        totals[0],
        totals[1],
        totals[2],
    )


def solution(mesh):
    placed = (
        P("gz", "gx", "gy"),
        P(None, "gz", "gx", "gy"),
        P("gz", "gx", "gy"),
        P(None, "gz", "gx", "gy"),
        P(),
        P(),
        P(),
    )
    return jax.shard_map(
        local,
        mesh=mesh,
        in_specs=placed,
        out_specs=(
            P(None, "gz", "gx", "gy"),
            P("gz", "gx", "gy"),
            P(None, "gz", "gx", "gy"),
            P("gz", "gx", "gy"),
            P(),
            P(),
            P(),
        ),
        check_vma=False,
    )
```

```python
import math

import jax
import jax.numpy as jnp
import numpy as np
from jax import lax
from jax.sharding import PartitionSpec as P

HEAT_RATIO = 1.4
THERMAL_DIFFUSE = 3.5
EDDY_SCALE = 0.5
TIME_STEP = 0.1
COMPACT_ALPHA = 1.0 / 3.0
COMPACT_NEAR = 14.0 / 9.0
COMPACT_FAR = 1.0 / 9.0
HIGHEST_PRECISION = lax.Precision.HIGHEST
NEAR_HALO = 2
NETWORK_PRECISION = lax.Precision.HIGH


def from_behind(value, axis, steps):
    count = lax.axis_size(axis)
    pairs = [(source, (source + steps) % count) for source in range(count)]
    return lax.ppermute(value, axis, pairs)


def prepare(mass_per_volume, flow_speed, pressure):
    energy = pressure / (HEAT_RATIO - 1.0) + 0.5 * mass_per_volume * jnp.sum(
        flow_speed * flow_speed, 0
    )
    state_now = jnp.concatenate(
        [mass_per_volume[None], mass_per_volume[None] * flow_speed, energy[None]], 0
    )
    scalars = jnp.concatenate([flow_speed, (pressure / mass_per_volume)[None]], 0)
    return (state_now, scalars)


def fluxes(mass_per_volume, flow_speed, pressure, upstream_cotangent, eddy_viscosity):
    energy = pressure / (HEAT_RATIO - 1.0) + 0.5 * mass_per_volume * jnp.sum(
        flow_speed * flow_speed, 0
    )
    attenuation_coefficient = mass_per_volume * eddy_viscosity
    stagnation_specific_energy = energy + pressure
    directions = []
    for traversal_axis in range(3):
        transported_array = flow_speed[traversal_axis]
        partition_parts = [mass_per_volume * transported_array]
        for coordinate_slot in range(3):
            mass_flux_array = (
                mass_per_volume * flow_speed[coordinate_slot] * transported_array
                - attenuation_coefficient * upstream_cotangent[traversal_axis, coordinate_slot]
            )
            if coordinate_slot == traversal_axis:
                mass_flux_array = mass_flux_array + pressure
            partition_parts.append(mass_flux_array)
        partition_parts.append(
            stagnation_specific_energy * transported_array
            - THERMAL_DIFFUSE * attenuation_coefficient * upstream_cotangent[traversal_axis, 3]
        )
        directions.append(jnp.stack(partition_parts))
    return jnp.stack(directions)


def viscosity(upstream_cotangent, inner_weight, middle_weight, outer_weight):
    features = upstream_cotangent[:, :3].reshape((9,) + upstream_cotangent.shape[2:])
    hidden = jnp.tanh(
        jnp.einsum("hc,czxy->hzxy", inner_weight, features, precision=NETWORK_PRECISION)
    )
    hidden = jnp.tanh(
        jnp.einsum("hk,kzxy->hzxy", middle_weight, hidden, precision=NETWORK_PRECISION)
    )
    output = jnp.einsum("h,hzxy->zxy", outer_weight, hidden, precision=NETWORK_PRECISION)
    return EDDY_SCALE * jax.nn.softplus(output)


def local_flux(
    density_in, velocity_in, pressure_in, upstream_cotangent, inner_in, middle_in, outer_in
):
    eddy_viscosity = viscosity(upstream_cotangent, inner_in, middle_in, outer_in)
    return fluxes(density_in, velocity_in, pressure_in, upstream_cotangent, eddy_viscosity)


def compact_tables(x_cells, line_length):
    eye = np.eye(line_length)
    system = eye + COMPACT_ALPHA * (np.roll(eye, 1, 1) + np.roll(eye, -1, 1))
    right = np.zeros((line_length, line_length))
    cells = np.arange(line_length)
    for offset, value in (
        (1, 0.5 * COMPACT_NEAR),
        (-1, -0.5 * COMPACT_NEAR),
        (2, 0.25 * COMPACT_FAR),
        (-2, -0.25 * COMPACT_FAR),
    ):
        right[cells, (cells + offset) % line_length] += value
    row = np.linalg.solve(system, right)[0]

    def coef(offset):
        return row[offset % line_length]

    ratio = (-1.0 + np.sqrt(1.0 - 4.0 * COMPACT_ALPHA**2)) / (2.0 * COMPACT_ALPHA)
    gain = coef(NEAR_HALO + 1) / ratio ** (NEAR_HALO + 1)
    n, h = x_cells, NEAR_HALO
    own = np.arange(n)
    send = np.zeros((2 * h + 4, n))
    for k in range(h):
        send[k, n - h + k] = 1.0
    send[h, : n - h] = ratio ** (n - own[: n - h])
    send[h + 1] = ratio ** (2 * n - own)
    for k in range(h):
        send[h + 2 + k, k] = 1.0
    send[2 * h + 2, h:] = ratio ** own[h:]
    send[2 * h + 3] = ratio ** (n + own)
    width = n + 2 * h + 4
    take = np.zeros((n, width))
    for i in range(n):
        take[i, 0] = -gain * ratio**i
        for k in range(h):
            take[i, 1 + k] = coef(-h + k - i)
        take[i, 1 + h] = -gain * ratio**i
        for m in range(n):
            take[i, 2 + h + m] = coef(m - i)
        for k in range(h):
            take[i, 2 + h + n + k] = coef(n + k - i)
        take[i, 2 + 2 * h + n] = gain * ratio ** (n - i)
        take[i, 3 + 2 * h + n] = gain * ratio ** (n - i)
    return send, take


def derive_x(fields):
    x_cells = fields.shape[2]
    groups = lax.axis_size("gx")
    h = NEAR_HALO
    send, take = compact_tables(x_cells, x_cells * groups)
    send = jnp.asarray(send, jnp.float32)
    take = jnp.asarray(take, jnp.float32)
    planes = jnp.einsum("pj,fzjy->fzpy", send, fields, precision=NETWORK_PRECISION)
    to_right = planes[:, :, : h + 1]
    to_right2 = planes[:, :, h + 1 : h + 2]
    to_left = planes[:, :, h + 2 : 2 * h + 3]
    to_left2 = planes[:, :, 2 * h + 3 :]
    from_left = from_behind(to_right, "gx", 1)
    from_left2 = from_behind(to_right2, "gx", 2)
    from_right = from_behind(to_left, "gx", -1)
    from_right2 = from_behind(to_left2, "gx", -2)
    received = jnp.concatenate([from_left2, from_left, from_right, from_right2], axis=2)
    take_own = take[:, h + 2 : h + 2 + x_cells]
    take_received = jnp.concatenate([take[:, : h + 2], take[:, h + 2 + x_cells :]], axis=1)
    own_part = jnp.einsum("ij,fzjy->fziy", take_own, fields, precision=NETWORK_PRECISION)
    return own_part + jnp.einsum(
        "ij,fzjy->fziy", take_received, received, precision=NETWORK_PRECISION
    )


def halo(block, axis, dim, width):
    count = lax.axis_size(axis)
    size = block.shape[dim]
    low_part = lax.slice_in_dim(block, size - width, size, axis=dim)
    high_part = lax.slice_in_dim(block, 0, width, axis=dim)
    if count == 2:
        both = from_behind(jnp.concatenate([low_part, high_part], axis=dim), axis, 1)
        low = lax.slice_in_dim(both, 0, width, axis=dim)
        high = lax.slice_in_dim(both, width, 2 * width, axis=dim)
    else:
        low = from_behind(low_part, axis, 1)
        high = from_behind(high_part, axis, -1)
    return jnp.concatenate([low, block, high], axis=dim)


def centered(extended, along_axis, margin, length):

    def shifted(offset):
        return lax.slice_in_dim(
            extended, margin + offset, margin + offset + length, axis=along_axis
        )

    return (
        45.0 * (shifted(1) - shifted(-1))
        - 9.0 * (shifted(2) - shifted(-2))
        + (shifted(3) - shifted(-3))
    ) / 60.0


def derive_y(fields):
    return centered(halo(fields, "gy", 3, 3), 3, 3, fields.shape[3])


def derive_z(fields):
    return centered(halo(fields, "gz", 1, 3), 1, 3, fields.shape[1])


def butterfly_sum(value, axis):
    count = lax.axis_size(axis)
    step = 1
    while step < count:
        if count % (2 * step) == 0:
            pairs = [(s, s ^ step) for s in range(count)]
            value = value + lax.ppermute(value, axis, pairs)
            step *= 2
        else:
            return lax.psum(value, axis)
    return value


def local(
    mass_per_volume, flow_speed, pressure, cotangent, weight_inner, weight_middle, weight_outer
):
    (state_now, scalars), prepare_pullback = jax.vjp(prepare, mass_per_volume, flow_speed, pressure)
    count = scalars.shape[0]
    first = jnp.concatenate([scalars, cotangent], 0)
    first_x = derive_x(first)
    first_y = derive_y(first)
    first_z = derive_z(first)
    gradients = jnp.stack([first_x[:count], first_y[:count], first_z[:count]])
    spread = jnp.stack([first_x[count:], first_y[count:], first_z[count:]])
    flux_all, flux_pullback = jax.vjp(
        local_flux,
        mass_per_volume,
        flow_speed,
        pressure,
        gradients,
        weight_inner,
        weight_middle,
        weight_outer,
    )
    pulled = flux_pullback(TIME_STEP * spread)
    gradient_bar = pulled[3]
    second_x = derive_x(jnp.concatenate([flux_all[0], gradient_bar[0]], 0))
    second_y = derive_y(jnp.concatenate([flux_all[1], gradient_bar[1]], 0))
    second_z = derive_z(jnp.concatenate([flux_all[2], gradient_bar[2]], 0))
    second = second_x + second_y + second_z
    states = state_now.shape[0]
    state_next = state_now - TIME_STEP * second[:states]
    scalar_bar = -second[states:]
    direct = prepare_pullback((cotangent, scalar_bar))
    weights = (pulled[4], pulled[5], pulled[6])
    flat = jnp.concatenate([w.reshape(-1) for w in weights])
    for axis in ("gz", "gy", "gx"):
        flat = butterfly_sum(flat, axis)
    cells_all = (
        mass_per_volume.size * lax.axis_size("gx") * lax.axis_size("gy") * lax.axis_size("gz")
    )
    factor = 1.0 / math.sqrt(cells_all)
    totals = []
    start = 0
    for w in weights:
        totals.append(flat[start : start + w.size].reshape(w.shape) * factor)
        start += w.size
    return (
        state_next,
        direct[0] + pulled[0],
        direct[1] + pulled[1],
        direct[2] + pulled[2],
        totals[0],
        totals[1],
        totals[2],
    )


def solution(mesh):
    placed = (
        P("gz", "gx", "gy"),
        P(None, "gz", "gx", "gy"),
        P("gz", "gx", "gy"),
        P(None, "gz", "gx", "gy"),
        P(),
        P(),
        P(),
    )
    return jax.shard_map(
        local,
        mesh=mesh,
        in_specs=placed,
        out_specs=(
            P(None, "gz", "gx", "gy"),
            P("gz", "gx", "gy"),
            P(None, "gz", "gx", "gy"),
            P("gz", "gx", "gy"),
            P(),
            P(),
            P(),
        ),
        check_vma=False,
    )
```

```python
import math

import jax
import jax.numpy as jnp
import numpy as np
from jax import lax
from jax.sharding import PartitionSpec as P

HEAT_RATIO = 1.4
THERMAL_DIFFUSE = 3.5
EDDY_SCALE = 0.5
TIME_STEP = 0.1
COMPACT_ALPHA = 1.0 / 3.0
COMPACT_NEAR = 14.0 / 9.0
COMPACT_FAR = 1.0 / 9.0
HIGHEST_PRECISION = lax.Precision.HIGHEST
NEAR_HALO = 2
NETWORK_PRECISION = lax.Precision.HIGH


def from_behind(value, axis, steps):
    count = lax.axis_size(axis)
    pairs = [(source, (source + steps) % count) for source in range(count)]
    return lax.ppermute(value, axis, pairs)


def prepare(mass_per_volume, flow_speed, pressure):
    energy = pressure / (HEAT_RATIO - 1.0) + 0.5 * mass_per_volume * jnp.sum(
        flow_speed * flow_speed, 0
    )
    state_now = jnp.concatenate(
        [mass_per_volume[None], mass_per_volume[None] * flow_speed, energy[None]], 0
    )
    scalars = jnp.concatenate([flow_speed, (pressure / mass_per_volume)[None]], 0)
    return (state_now, scalars)


def fluxes(mass_per_volume, flow_speed, pressure, upstream_cotangent, eddy_viscosity):
    energy = pressure / (HEAT_RATIO - 1.0) + 0.5 * mass_per_volume * jnp.sum(
        flow_speed * flow_speed, 0
    )
    attenuation_coefficient = mass_per_volume * eddy_viscosity
    stagnation_specific_energy = energy + pressure
    directions = []
    for traversal_axis in range(3):
        transported_array = flow_speed[traversal_axis]
        partition_parts = [mass_per_volume * transported_array]
        for coordinate_slot in range(3):
            mass_flux_array = (
                mass_per_volume * flow_speed[coordinate_slot] * transported_array
                - attenuation_coefficient * upstream_cotangent[traversal_axis, coordinate_slot]
            )
            if coordinate_slot == traversal_axis:
                mass_flux_array = mass_flux_array + pressure
            partition_parts.append(mass_flux_array)
        partition_parts.append(
            stagnation_specific_energy * transported_array
            - THERMAL_DIFFUSE * attenuation_coefficient * upstream_cotangent[traversal_axis, 3]
        )
        directions.append(jnp.stack(partition_parts))
    return jnp.stack(directions)


def viscosity(upstream_cotangent, inner_weight, middle_weight, outer_weight):
    features = upstream_cotangent[:, :3].reshape((9,) + upstream_cotangent.shape[2:])
    hidden = jnp.tanh(
        jnp.einsum("hc,czxy->hzxy", inner_weight, features, precision=NETWORK_PRECISION)
    )
    hidden = jnp.tanh(
        jnp.einsum("hk,kzxy->hzxy", middle_weight, hidden, precision=NETWORK_PRECISION)
    )
    output = jnp.einsum("h,hzxy->zxy", outer_weight, hidden, precision=NETWORK_PRECISION)
    return EDDY_SCALE * jax.nn.softplus(output)


def local_flux(
    density_in, velocity_in, pressure_in, upstream_cotangent, inner_in, middle_in, outer_in
):
    eddy_viscosity = viscosity(upstream_cotangent, inner_in, middle_in, outer_in)
    return fluxes(density_in, velocity_in, pressure_in, upstream_cotangent, eddy_viscosity)


def compact_tables(x_cells, line_length):
    eye = np.eye(line_length)
    system = eye + COMPACT_ALPHA * (np.roll(eye, 1, 1) + np.roll(eye, -1, 1))
    right = np.zeros((line_length, line_length))
    cells = np.arange(line_length)
    for offset, value in (
        (1, 0.5 * COMPACT_NEAR),
        (-1, -0.5 * COMPACT_NEAR),
        (2, 0.25 * COMPACT_FAR),
        (-2, -0.25 * COMPACT_FAR),
    ):
        right[cells, (cells + offset) % line_length] += value
    row = np.linalg.solve(system, right)[0]

    def coef(offset):
        return row[offset % line_length]

    ratio = (-1.0 + np.sqrt(1.0 - 4.0 * COMPACT_ALPHA**2)) / (2.0 * COMPACT_ALPHA)
    gain = coef(NEAR_HALO + 1) / ratio ** (NEAR_HALO + 1)
    n, h = x_cells, NEAR_HALO
    own = np.arange(n)
    send = np.zeros((2 * h + 4, n))
    for k in range(h):
        send[k, n - h + k] = 1.0
    send[h, : n - h] = ratio ** (n - own[: n - h])
    send[h + 1] = ratio ** (2 * n - own)
    for k in range(h):
        send[h + 2 + k, k] = 1.0
    send[2 * h + 2, h:] = ratio ** own[h:]
    send[2 * h + 3] = ratio ** (n + own)
    width = n + 2 * h + 4
    take = np.zeros((n, width))
    for i in range(n):
        take[i, 0] = -gain * ratio**i
        for k in range(h):
            take[i, 1 + k] = coef(-h + k - i)
        take[i, 1 + h] = -gain * ratio**i
        for m in range(n):
            take[i, 2 + h + m] = coef(m - i)
        for k in range(h):
            take[i, 2 + h + n + k] = coef(n + k - i)
        take[i, 2 + 2 * h + n] = gain * ratio ** (n - i)
        take[i, 3 + 2 * h + n] = gain * ratio ** (n - i)
    return send, take


def derive_x(fields):
    x_cells = fields.shape[2]
    groups = lax.axis_size("gx")
    h = NEAR_HALO
    send, take = compact_tables(x_cells, x_cells * groups)
    send = jnp.asarray(send, jnp.float32)
    take = jnp.asarray(take, jnp.float32)
    planes = jnp.einsum("pj,fzjy->fzpy", send, fields, precision=NETWORK_PRECISION)
    to_right = planes[:, :, : h + 1]
    to_right2 = planes[:, :, h + 1 : h + 2]
    to_left = planes[:, :, h + 2 : 2 * h + 3]
    to_left2 = planes[:, :, 2 * h + 3 :]
    from_left = from_behind(to_right, "gx", 1)
    from_left2 = from_behind(to_right2, "gx", 2)
    from_right = from_behind(to_left, "gx", -1)
    from_right2 = from_behind(to_left2, "gx", -2)
    received = jnp.concatenate([from_left2, from_left, from_right, from_right2], axis=2)
    take_own = take[:, h + 2 : h + 2 + x_cells]
    take_received = jnp.concatenate([take[:, : h + 2], take[:, h + 2 + x_cells :]], axis=1)
    own_part = jnp.einsum("ij,fzjy->fziy", take_own, fields, precision=NETWORK_PRECISION)
    return own_part + jnp.einsum(
        "ij,fzjy->fziy", take_received, received, precision=NETWORK_PRECISION
    )


def halo(block, axis, dim, width):
    count = lax.axis_size(axis)
    size = block.shape[dim]
    low_part = lax.slice_in_dim(block, size - width, size, axis=dim)
    high_part = lax.slice_in_dim(block, 0, width, axis=dim)
    if count == 2:
        both = from_behind(jnp.concatenate([low_part, high_part], axis=dim), axis, 1)
        low = lax.slice_in_dim(both, 0, width, axis=dim)
        high = lax.slice_in_dim(both, width, 2 * width, axis=dim)
    else:
        low = from_behind(low_part, axis, 1)
        high = from_behind(high_part, axis, -1)
    return jnp.concatenate([low, block, high], axis=dim)


def centered(extended, along_axis, margin, length):

    def shifted(offset):
        return lax.slice_in_dim(
            extended, margin + offset, margin + offset + length, axis=along_axis
        )

    return (
        45.0 * (shifted(1) - shifted(-1))
        - 9.0 * (shifted(2) - shifted(-2))
        + (shifted(3) - shifted(-3))
    ) / 60.0


def derive_y(fields):
    return centered(halo(fields, "gy", 3, 3), 3, 3, fields.shape[3])


def derive_z(fields):
    return centered(halo(fields, "gz", 1, 3), 1, 3, fields.shape[1])


def butterfly_sum(value, axis):
    count = lax.axis_size(axis)
    step = 1
    while step < count:
        if count % (2 * step) == 0:
            pairs = [(s, s ^ step) for s in range(count)]
            value = value + lax.ppermute(value, axis, pairs)
            step *= 2
        else:
            return lax.psum(value, axis)
    return value


def local(
    mass_per_volume, flow_speed, pressure, cotangent, weight_inner, weight_middle, weight_outer
):
    (state_now, scalars), prepare_pullback = jax.vjp(prepare, mass_per_volume, flow_speed, pressure)
    count = scalars.shape[0]
    first = jnp.concatenate([scalars, cotangent], 0)
    first_x = derive_x(first)
    first_y = derive_y(first)
    first_z = derive_z(first)
    gradients = jnp.stack([first_x[:count], first_y[:count], first_z[:count]])
    spread = jnp.stack([first_x[count:], first_y[count:], first_z[count:]])
    flux_all, flux_pullback = jax.vjp(
        local_flux,
        mass_per_volume,
        flow_speed,
        pressure,
        gradients,
        weight_inner,
        weight_middle,
        weight_outer,
    )
    pulled = flux_pullback(TIME_STEP * spread)
    gradient_bar = pulled[3]
    second_x = derive_x(jnp.concatenate([flux_all[0], gradient_bar[0]], 0))
    second_y = derive_y(jnp.concatenate([flux_all[1], gradient_bar[1]], 0))
    along_z = jnp.concatenate([flux_all[2], gradient_bar[2]], 0)
    weights = (pulled[4], pulled[5], pulled[6])
    flat = jnp.concatenate([w.reshape(-1) for w in weights])
    fields, depth, rows, lanes = along_z.shape
    slab = fields * rows * lanes
    if lax.axis_size("gz") == 2 and flat.size <= slab and depth >= 3:
        packed = jnp.pad(flat, (0, slab - flat.size)).reshape(fields, 1, rows, lanes)
        sent = jnp.concatenate([along_z[:, depth - 3 :], along_z[:, :3], packed], axis=1)
        got = from_behind(sent, "gz", 1)
        extended_z = jnp.concatenate([got[:, :3], along_z, got[:, 3:6]], axis=1)
        second_z = centered(extended_z, 1, 3, depth)
        flat = flat + got[:, 6:].reshape(-1)[: flat.size]
        sum_axes = ("gy", "gx")
    else:
        second_z = derive_z(along_z)
        sum_axes = ("gz", "gy", "gx")
    second = second_x + second_y + second_z
    states = state_now.shape[0]
    state_next = state_now - TIME_STEP * second[:states]
    scalar_bar = -second[states:]
    direct = prepare_pullback((cotangent, scalar_bar))
    for axis in sum_axes:
        flat = butterfly_sum(flat, axis)
    cells_all = (
        mass_per_volume.size * lax.axis_size("gx") * lax.axis_size("gy") * lax.axis_size("gz")
    )
    factor = 1.0 / math.sqrt(cells_all)
    totals = []
    start = 0
    for w in weights:
        totals.append(flat[start : start + w.size].reshape(w.shape) * factor)
        start += w.size
    return (
        state_next,
        direct[0] + pulled[0],
        direct[1] + pulled[1],
        direct[2] + pulled[2],
        totals[0],
        totals[1],
        totals[2],
    )


def solution(mesh):
    placed = (
        P("gz", "gx", "gy"),
        P(None, "gz", "gx", "gy"),
        P("gz", "gx", "gy"),
        P(None, "gz", "gx", "gy"),
        P(),
        P(),
        P(),
    )
    return jax.shard_map(
        local,
        mesh=mesh,
        in_specs=placed,
        out_specs=(
            P(None, "gz", "gx", "gy"),
            P("gz", "gx", "gy"),
            P(None, "gz", "gx", "gy"),
            P("gz", "gx", "gy"),
            P(),
            P(),
            P(),
        ),
        check_vma=False,
    )
```

```python
import math

import jax
import jax.numpy as jnp
import numpy as np
from jax import lax
from jax.sharding import PartitionSpec as P

HEAT_RATIO = 1.4
THERMAL_DIFFUSE = 3.5
EDDY_SCALE = 0.5
TIME_STEP = 0.1
COMPACT_ALPHA = 1.0 / 3.0
COMPACT_NEAR = 14.0 / 9.0
COMPACT_FAR = 1.0 / 9.0
HIGHEST_PRECISION = lax.Precision.HIGHEST
NEAR_HALO = 2
NETWORK_PRECISION = lax.Precision.HIGH


def from_behind(value, axis, steps):
    count = lax.axis_size(axis)
    pairs = [(source, (source + steps) % count) for source in range(count)]
    return lax.ppermute(value, axis, pairs)


def prepare(mass_per_volume, flow_speed, pressure):
    energy = pressure / (HEAT_RATIO - 1.0) + 0.5 * mass_per_volume * jnp.sum(
        flow_speed * flow_speed, 0
    )
    state_now = jnp.concatenate(
        [mass_per_volume[None], mass_per_volume[None] * flow_speed, energy[None]], 0
    )
    scalars = jnp.concatenate([flow_speed, (pressure / mass_per_volume)[None]], 0)
    return (state_now, scalars)


def fluxes(mass_per_volume, flow_speed, pressure, upstream_cotangent, eddy_viscosity):
    energy = pressure / (HEAT_RATIO - 1.0) + 0.5 * mass_per_volume * jnp.sum(
        flow_speed * flow_speed, 0
    )
    attenuation_coefficient = mass_per_volume * eddy_viscosity
    stagnation_specific_energy = energy + pressure
    directions = []
    for traversal_axis in range(3):
        transported_array = flow_speed[traversal_axis]
        partition_parts = [mass_per_volume * transported_array]
        for coordinate_slot in range(3):
            mass_flux_array = (
                mass_per_volume * flow_speed[coordinate_slot] * transported_array
                - attenuation_coefficient * upstream_cotangent[traversal_axis, coordinate_slot]
            )
            if coordinate_slot == traversal_axis:
                mass_flux_array = mass_flux_array + pressure
            partition_parts.append(mass_flux_array)
        partition_parts.append(
            stagnation_specific_energy * transported_array
            - THERMAL_DIFFUSE * attenuation_coefficient * upstream_cotangent[traversal_axis, 3]
        )
        directions.append(jnp.stack(partition_parts))
    return jnp.stack(directions)


def viscosity(upstream_cotangent, inner_weight, middle_weight, outer_weight):
    features = upstream_cotangent[:, :3].reshape((9,) + upstream_cotangent.shape[2:])
    hidden = jnp.tanh(
        jnp.einsum("hc,czxy->hzxy", inner_weight, features, precision=NETWORK_PRECISION)
    )
    hidden = jnp.tanh(
        jnp.einsum("hk,kzxy->hzxy", middle_weight, hidden, precision=NETWORK_PRECISION)
    )
    output = jnp.einsum("h,hzxy->zxy", outer_weight, hidden, precision=NETWORK_PRECISION)
    return EDDY_SCALE * jax.nn.softplus(output)


def local_flux(
    density_in, velocity_in, pressure_in, upstream_cotangent, inner_in, middle_in, outer_in
):
    eddy_viscosity = viscosity(upstream_cotangent, inner_in, middle_in, outer_in)
    return fluxes(density_in, velocity_in, pressure_in, upstream_cotangent, eddy_viscosity)


def compact_tables(x_cells, line_length):
    eye = np.eye(line_length)
    system = eye + COMPACT_ALPHA * (np.roll(eye, 1, 1) + np.roll(eye, -1, 1))
    right = np.zeros((line_length, line_length))
    cells = np.arange(line_length)
    for offset, value in (
        (1, 0.5 * COMPACT_NEAR),
        (-1, -0.5 * COMPACT_NEAR),
        (2, 0.25 * COMPACT_FAR),
        (-2, -0.25 * COMPACT_FAR),
    ):
        right[cells, (cells + offset) % line_length] += value
    row = np.linalg.solve(system, right)[0]

    def coef(offset):
        return row[offset % line_length]

    ratio = (-1.0 + np.sqrt(1.0 - 4.0 * COMPACT_ALPHA**2)) / (2.0 * COMPACT_ALPHA)
    gain = coef(NEAR_HALO + 1) / ratio ** (NEAR_HALO + 1)
    n, h = x_cells, NEAR_HALO
    own = np.arange(n)
    send = np.zeros((2 * h + 4, n))
    for k in range(h):
        send[k, n - h + k] = 1.0
    send[h, : n - h] = ratio ** (n - own[: n - h])
    send[h + 1] = ratio ** (2 * n - own)
    for k in range(h):
        send[h + 2 + k, k] = 1.0
    send[2 * h + 2, h:] = ratio ** own[h:]
    send[2 * h + 3] = ratio ** (n + own)
    width = n + 2 * h + 4
    take = np.zeros((n, width))
    for i in range(n):
        take[i, 0] = -gain * ratio**i
        for k in range(h):
            take[i, 1 + k] = coef(-h + k - i)
        take[i, 1 + h] = -gain * ratio**i
        for m in range(n):
            take[i, 2 + h + m] = coef(m - i)
        for k in range(h):
            take[i, 2 + h + n + k] = coef(n + k - i)
        take[i, 2 + 2 * h + n] = gain * ratio ** (n - i)
        take[i, 3 + 2 * h + n] = gain * ratio ** (n - i)
    return send, take


def derive_x(fields):
    x_cells = fields.shape[2]
    groups = lax.axis_size("gx")
    h = NEAR_HALO
    send, take = compact_tables(x_cells, x_cells * groups)
    send = jnp.asarray(send, jnp.float32)
    take = jnp.asarray(take, jnp.float32)
    planes = jnp.einsum("pj,fzjy->fzpy", send, fields, precision=NETWORK_PRECISION)
    to_right = planes[:, :, : h + 1]
    to_right2 = planes[:, :, h + 1 : h + 2]
    to_left = planes[:, :, h + 2 : 2 * h + 3]
    to_left2 = planes[:, :, 2 * h + 3 :]
    from_left = from_behind(to_right, "gx", 1)
    from_left2 = from_behind(to_right2, "gx", 2)
    from_right = from_behind(to_left, "gx", -1)
    from_right2 = from_behind(to_left2, "gx", -2)
    received = jnp.concatenate([from_left2, from_left, from_right, from_right2], axis=2)
    take_own = take[:, h + 2 : h + 2 + x_cells]
    take_received = jnp.concatenate([take[:, : h + 2], take[:, h + 2 + x_cells :]], axis=1)
    own_part = jnp.einsum("ij,fzjy->fziy", take_own, fields, precision=NETWORK_PRECISION)
    for j in range(received.shape[2]):
        own_part = own_part + take_received[:, j][None, None, :, None] * received[:, :, j : j + 1]
    return own_part


def halo(block, axis, dim, width):
    count = lax.axis_size(axis)
    size = block.shape[dim]
    low_part = lax.slice_in_dim(block, size - width, size, axis=dim)
    high_part = lax.slice_in_dim(block, 0, width, axis=dim)
    if count == 2:
        both = from_behind(jnp.concatenate([low_part, high_part], axis=dim), axis, 1)
        low = lax.slice_in_dim(both, 0, width, axis=dim)
        high = lax.slice_in_dim(both, width, 2 * width, axis=dim)
    else:
        low = from_behind(low_part, axis, 1)
        high = from_behind(high_part, axis, -1)
    return jnp.concatenate([low, block, high], axis=dim)


def centered(extended, along_axis, margin, length):

    def shifted(offset):
        return lax.slice_in_dim(
            extended, margin + offset, margin + offset + length, axis=along_axis
        )

    return (
        45.0 * (shifted(1) - shifted(-1))
        - 9.0 * (shifted(2) - shifted(-2))
        + (shifted(3) - shifted(-3))
    ) / 60.0


def derive_y(fields):
    return centered(halo(fields, "gy", 3, 3), 3, 3, fields.shape[3])


def derive_z(fields):
    return centered(halo(fields, "gz", 1, 3), 1, 3, fields.shape[1])


def butterfly_sum(value, axis):
    count = lax.axis_size(axis)
    step = 1
    while step < count:
        if count % (2 * step) == 0:
            pairs = [(s, s ^ step) for s in range(count)]
            value = value + lax.ppermute(value, axis, pairs)
            step *= 2
        else:
            return lax.psum(value, axis)
    return value


def local(
    mass_per_volume, flow_speed, pressure, cotangent, weight_inner, weight_middle, weight_outer
):
    (state_now, scalars), prepare_pullback = jax.vjp(prepare, mass_per_volume, flow_speed, pressure)
    count = scalars.shape[0]
    first = jnp.concatenate([scalars, cotangent], 0)
    first_x = derive_x(first)
    first_y = derive_y(first)
    first_z = derive_z(first)
    gradients = jnp.stack([first_x[:count], first_y[:count], first_z[:count]])
    spread = jnp.stack([first_x[count:], first_y[count:], first_z[count:]])
    flux_all, flux_pullback = jax.vjp(
        local_flux,
        mass_per_volume,
        flow_speed,
        pressure,
        gradients,
        weight_inner,
        weight_middle,
        weight_outer,
    )
    pulled = flux_pullback(TIME_STEP * spread)
    gradient_bar = pulled[3]
    second_x = derive_x(jnp.concatenate([flux_all[0], gradient_bar[0]], 0))
    second_y = derive_y(jnp.concatenate([flux_all[1], gradient_bar[1]], 0))
    second_z = derive_z(jnp.concatenate([flux_all[2], gradient_bar[2]], 0))
    second = second_x + second_y + second_z
    states = state_now.shape[0]
    state_next = state_now - TIME_STEP * second[:states]
    scalar_bar = -second[states:]
    direct = prepare_pullback((cotangent, scalar_bar))
    weights = (pulled[4], pulled[5], pulled[6])
    flat = jnp.concatenate([w.reshape(-1) for w in weights])
    for axis in ("gz", "gy", "gx"):
        flat = butterfly_sum(flat, axis)
    cells_all = (
        mass_per_volume.size * lax.axis_size("gx") * lax.axis_size("gy") * lax.axis_size("gz")
    )
    factor = 1.0 / math.sqrt(cells_all)
    totals = []
    start = 0
    for w in weights:
        totals.append(flat[start : start + w.size].reshape(w.shape) * factor)
        start += w.size
    return (
        state_next,
        direct[0] + pulled[0],
        direct[1] + pulled[1],
        direct[2] + pulled[2],
        totals[0],
        totals[1],
        totals[2],
    )


def solution(mesh):
    placed = (
        P("gz", "gx", "gy"),
        P(None, "gz", "gx", "gy"),
        P("gz", "gx", "gy"),
        P(None, "gz", "gx", "gy"),
        P(),
        P(),
        P(),
    )
    return jax.shard_map(
        local,
        mesh=mesh,
        in_specs=placed,
        out_specs=(
            P(None, "gz", "gx", "gy"),
            P("gz", "gx", "gy"),
            P(None, "gz", "gx", "gy"),
            P("gz", "gx", "gy"),
            P(),
            P(),
            P(),
        ),
        check_vma=False,
    )
```

```python
import math

import jax
import jax.numpy as jnp
import numpy as np
from jax import lax
from jax.sharding import PartitionSpec as P

HEAT_RATIO = 1.4
THERMAL_DIFFUSE = 3.5
EDDY_SCALE = 0.5
TIME_STEP = 0.1
COMPACT_ALPHA = 1.0 / 3.0
COMPACT_NEAR = 14.0 / 9.0
COMPACT_FAR = 1.0 / 9.0
HIGHEST_PRECISION = lax.Precision.HIGHEST
NEAR_HALO = 2
NETWORK_PRECISION = lax.Precision.HIGH


def from_behind(value, axis, steps):
    count = lax.axis_size(axis)
    pairs = [(source, (source + steps) % count) for source in range(count)]
    return lax.ppermute(value, axis, pairs)


def prepare(mass_per_volume, flow_speed, pressure):
    energy = pressure / (HEAT_RATIO - 1.0) + 0.5 * mass_per_volume * jnp.sum(
        flow_speed * flow_speed, 0
    )
    state_now = jnp.concatenate(
        [mass_per_volume[None], mass_per_volume[None] * flow_speed, energy[None]], 0
    )
    scalars = jnp.concatenate([flow_speed, (pressure / mass_per_volume)[None]], 0)
    return (state_now, scalars)


def fluxes(mass_per_volume, flow_speed, pressure, upstream_cotangent, eddy_viscosity):
    energy = pressure / (HEAT_RATIO - 1.0) + 0.5 * mass_per_volume * jnp.sum(
        flow_speed * flow_speed, 0
    )
    attenuation_coefficient = mass_per_volume * eddy_viscosity
    stagnation_specific_energy = energy + pressure
    directions = []
    for traversal_axis in range(3):
        transported_array = flow_speed[traversal_axis]
        partition_parts = [mass_per_volume * transported_array]
        for coordinate_slot in range(3):
            mass_flux_array = (
                mass_per_volume * flow_speed[coordinate_slot] * transported_array
                - attenuation_coefficient * upstream_cotangent[traversal_axis, coordinate_slot]
            )
            if coordinate_slot == traversal_axis:
                mass_flux_array = mass_flux_array + pressure
            partition_parts.append(mass_flux_array)
        partition_parts.append(
            stagnation_specific_energy * transported_array
            - THERMAL_DIFFUSE * attenuation_coefficient * upstream_cotangent[traversal_axis, 3]
        )
        directions.append(jnp.stack(partition_parts))
    return jnp.stack(directions)


def viscosity(upstream_cotangent, inner_weight, middle_weight, outer_weight):
    features = upstream_cotangent[:, :3].reshape((9,) + upstream_cotangent.shape[2:])
    hidden = jnp.tanh(
        jnp.einsum("hc,czxy->hzxy", inner_weight, features, precision=NETWORK_PRECISION)
    )
    hidden = jnp.tanh(
        jnp.einsum("hk,kzxy->hzxy", middle_weight, hidden, precision=NETWORK_PRECISION)
    )
    output = jnp.einsum("h,hzxy->zxy", outer_weight, hidden, precision=NETWORK_PRECISION)
    return EDDY_SCALE * jax.nn.softplus(output)


def local_flux(
    density_in, velocity_in, pressure_in, upstream_cotangent, inner_in, middle_in, outer_in
):
    eddy_viscosity = viscosity(upstream_cotangent, inner_in, middle_in, outer_in)
    return fluxes(density_in, velocity_in, pressure_in, upstream_cotangent, eddy_viscosity)


def compact_tables(x_cells, line_length):
    eye = np.eye(line_length)
    system = eye + COMPACT_ALPHA * (np.roll(eye, 1, 1) + np.roll(eye, -1, 1))
    right = np.zeros((line_length, line_length))
    cells = np.arange(line_length)
    for offset, value in (
        (1, 0.5 * COMPACT_NEAR),
        (-1, -0.5 * COMPACT_NEAR),
        (2, 0.25 * COMPACT_FAR),
        (-2, -0.25 * COMPACT_FAR),
    ):
        right[cells, (cells + offset) % line_length] += value
    row = np.linalg.solve(system, right)[0]

    def coef(offset):
        return row[offset % line_length]

    ratio = (-1.0 + np.sqrt(1.0 - 4.0 * COMPACT_ALPHA**2)) / (2.0 * COMPACT_ALPHA)
    gain = coef(NEAR_HALO + 1) / ratio ** (NEAR_HALO + 1)
    n, h = x_cells, NEAR_HALO
    own = np.arange(n)
    send = np.zeros((2 * h + 4, n))
    for k in range(h):
        send[k, n - h + k] = 1.0
    send[h, : n - h] = ratio ** (n - own[: n - h])
    send[h + 1] = ratio ** (2 * n - own)
    for k in range(h):
        send[h + 2 + k, k] = 1.0
    send[2 * h + 2, h:] = ratio ** own[h:]
    send[2 * h + 3] = ratio ** (n + own)
    width = n + 2 * h + 4
    take = np.zeros((n, width))
    for i in range(n):
        take[i, 0] = -gain * ratio**i
        for k in range(h):
            take[i, 1 + k] = coef(-h + k - i)
        take[i, 1 + h] = -gain * ratio**i
        for m in range(n):
            take[i, 2 + h + m] = coef(m - i)
        for k in range(h):
            take[i, 2 + h + n + k] = coef(n + k - i)
        take[i, 2 + 2 * h + n] = gain * ratio ** (n - i)
        take[i, 3 + 2 * h + n] = gain * ratio ** (n - i)
    return send, take


def derive_x(fields):
    x_cells = fields.shape[2]
    groups = lax.axis_size("gx")
    h = NEAR_HALO
    send, take = compact_tables(x_cells, x_cells * groups)
    send = jnp.asarray(send, jnp.float32)
    take = jnp.asarray(take, jnp.float32)
    planes = jnp.einsum("pj,fzjy->fzpy", send, fields, precision=NETWORK_PRECISION)
    to_right = planes[:, :, : h + 1]
    to_right2 = planes[:, :, h + 1 : h + 2]
    to_left = planes[:, :, h + 2 : 2 * h + 3]
    to_left2 = planes[:, :, 2 * h + 3 :]
    from_left = from_behind(to_right, "gx", 1)
    from_left2 = from_behind(to_right2, "gx", 2)
    from_right = from_behind(to_left, "gx", -1)
    from_right2 = from_behind(to_left2, "gx", -2)
    received = jnp.concatenate([from_left2, from_left, from_right, from_right2], axis=2)
    take_own = take[:, h + 2 : h + 2 + x_cells]
    take_received = jnp.concatenate([take[:, : h + 2], take[:, h + 2 + x_cells :]], axis=1)
    own_part = jnp.einsum("ij,fzjy->fziy", take_own, fields, precision=NETWORK_PRECISION)
    return own_part + jnp.einsum(
        "ij,fzjy->fziy", take_received, received, precision=NETWORK_PRECISION
    )


def halo(block, axis, dim, width):
    count = lax.axis_size(axis)
    size = block.shape[dim]
    low_part = lax.slice_in_dim(block, size - width, size, axis=dim)
    high_part = lax.slice_in_dim(block, 0, width, axis=dim)
    if count == 2:
        both = from_behind(jnp.concatenate([low_part, high_part], axis=dim), axis, 1)
        low = lax.slice_in_dim(both, 0, width, axis=dim)
        high = lax.slice_in_dim(both, width, 2 * width, axis=dim)
    else:
        low = from_behind(low_part, axis, 1)
        high = from_behind(high_part, axis, -1)
    return jnp.concatenate([low, block, high], axis=dim)


def centered(extended, along_axis, margin, length):

    def shifted(offset):
        return lax.slice_in_dim(
            extended, margin + offset, margin + offset + length, axis=along_axis
        )

    return (
        45.0 * (shifted(1) - shifted(-1))
        - 9.0 * (shifted(2) - shifted(-2))
        + (shifted(3) - shifted(-3))
    ) / 60.0


def derive_y(fields):
    return centered(halo(fields, "gy", 3, 3), 3, 3, fields.shape[3])


def derive_z(fields):
    return centered(halo(fields, "gz", 1, 3), 1, 3, fields.shape[1])


def butterfly_sum(value, axis):
    count = lax.axis_size(axis)
    step = 1
    while step < count:
        if count % (2 * step) == 0:
            pairs = [(s, s ^ step) for s in range(count)]
            value = value + lax.ppermute(value, axis, pairs)
            step *= 2
        else:
            return lax.psum(value, axis)
    return value


def local(
    mass_per_volume, flow_speed, pressure, cotangent, weight_inner, weight_middle, weight_outer
):
    (state_now, scalars), prepare_pullback = jax.vjp(prepare, mass_per_volume, flow_speed, pressure)
    count = scalars.shape[0]
    first = jnp.concatenate([scalars, cotangent], 0)
    first_x = derive_x(first)
    first_y = derive_y(first)
    first_z = derive_z(first)
    gradients = jnp.stack([first_x[:count], first_y[:count], first_z[:count]])
    spread = jnp.stack([first_x[count:], first_y[count:], first_z[count:]])
    flux_all, flux_pullback = jax.vjp(
        local_flux,
        mass_per_volume,
        flow_speed,
        pressure,
        gradients,
        weight_inner,
        weight_middle,
        weight_outer,
    )
    pulled = flux_pullback(TIME_STEP * spread)
    gradient_bar = pulled[3]
    second_x = derive_x(jnp.concatenate([flux_all[0], gradient_bar[0]], 0))
    second_y = derive_y(jnp.concatenate([flux_all[1], gradient_bar[1]], 0))
    second_z = derive_z(jnp.concatenate([flux_all[2], gradient_bar[2]], 0))
    second = second_x + second_y + second_z
    states = state_now.shape[0]
    state_next = state_now - TIME_STEP * second[:states]
    scalar_bar = -second[states:]
    direct = prepare_pullback((cotangent, scalar_bar))
    weights = (pulled[4], pulled[5], pulled[6])
    flat = jnp.concatenate([w.reshape(-1) for w in weights])
    for axis in ("gx", "gy", "gz"):
        flat = butterfly_sum(flat, axis)
    cells_all = (
        mass_per_volume.size * lax.axis_size("gx") * lax.axis_size("gy") * lax.axis_size("gz")
    )
    factor = 1.0 / math.sqrt(cells_all)
    totals = []
    start = 0
    for w in weights:
        totals.append(flat[start : start + w.size].reshape(w.shape) * factor)
        start += w.size
    return (
        state_next,
        direct[0] + pulled[0],
        direct[1] + pulled[1],
        direct[2] + pulled[2],
        totals[0],
        totals[1],
        totals[2],
    )


def solution(mesh):
    placed = (
        P("gz", "gx", "gy"),
        P(None, "gz", "gx", "gy"),
        P("gz", "gx", "gy"),
        P(None, "gz", "gx", "gy"),
        P(),
        P(),
        P(),
    )
    return jax.shard_map(
        local,
        mesh=mesh,
        in_specs=placed,
        out_specs=(
            P(None, "gz", "gx", "gy"),
            P("gz", "gx", "gy"),
            P(None, "gz", "gx", "gy"),
            P("gz", "gx", "gy"),
            P(),
            P(),
            P(),
        ),
        check_vma=False,
    )
```

```python
import math

import jax
import jax.numpy as jnp
import numpy as np
from jax import lax
from jax.sharding import PartitionSpec as P

HEAT_RATIO = 1.4
THERMAL_DIFFUSE = 3.5
EDDY_SCALE = 0.5
TIME_STEP = 0.1
COMPACT_ALPHA = 1.0 / 3.0
COMPACT_NEAR = 14.0 / 9.0
COMPACT_FAR = 1.0 / 9.0
HIGHEST_PRECISION = lax.Precision.HIGHEST
NEAR_HALO = 1
NETWORK_PRECISION = lax.Precision.HIGH


def from_behind(value, axis, steps):
    count = lax.axis_size(axis)
    pairs = [(source, (source + steps) % count) for source in range(count)]
    return lax.ppermute(value, axis, pairs)


def prepare(mass_per_volume, flow_speed, pressure):
    energy = pressure / (HEAT_RATIO - 1.0) + 0.5 * mass_per_volume * jnp.sum(
        flow_speed * flow_speed, 0
    )
    state_now = jnp.concatenate(
        [mass_per_volume[None], mass_per_volume[None] * flow_speed, energy[None]], 0
    )
    scalars = jnp.concatenate([flow_speed, (pressure / mass_per_volume)[None]], 0)
    return (state_now, scalars)


def fluxes(mass_per_volume, flow_speed, pressure, upstream_cotangent, eddy_viscosity):
    energy = pressure / (HEAT_RATIO - 1.0) + 0.5 * mass_per_volume * jnp.sum(
        flow_speed * flow_speed, 0
    )
    attenuation_coefficient = mass_per_volume * eddy_viscosity
    stagnation_specific_energy = energy + pressure
    directions = []
    for traversal_axis in range(3):
        transported_array = flow_speed[traversal_axis]
        partition_parts = [mass_per_volume * transported_array]
        for coordinate_slot in range(3):
            mass_flux_array = (
                mass_per_volume * flow_speed[coordinate_slot] * transported_array
                - attenuation_coefficient * upstream_cotangent[traversal_axis, coordinate_slot]
            )
            if coordinate_slot == traversal_axis:
                mass_flux_array = mass_flux_array + pressure
            partition_parts.append(mass_flux_array)
        partition_parts.append(
            stagnation_specific_energy * transported_array
            - THERMAL_DIFFUSE * attenuation_coefficient * upstream_cotangent[traversal_axis, 3]
        )
        directions.append(jnp.stack(partition_parts))
    return jnp.stack(directions)


def viscosity(upstream_cotangent, inner_weight, middle_weight, outer_weight):
    features = upstream_cotangent[:, :3].reshape((9,) + upstream_cotangent.shape[2:])
    hidden = jnp.tanh(
        jnp.einsum("hc,czxy->hzxy", inner_weight, features, precision=NETWORK_PRECISION)
    )
    hidden = jnp.tanh(
        jnp.einsum("hk,kzxy->hzxy", middle_weight, hidden, precision=NETWORK_PRECISION)
    )
    output = jnp.einsum("h,hzxy->zxy", outer_weight, hidden, precision=NETWORK_PRECISION)
    return EDDY_SCALE * jax.nn.softplus(output)


def local_flux(
    density_in, velocity_in, pressure_in, upstream_cotangent, inner_in, middle_in, outer_in
):
    eddy_viscosity = viscosity(upstream_cotangent, inner_in, middle_in, outer_in)
    return fluxes(density_in, velocity_in, pressure_in, upstream_cotangent, eddy_viscosity)


def compact_tables(x_cells, line_length):
    eye = np.eye(line_length)
    system = eye + COMPACT_ALPHA * (np.roll(eye, 1, 1) + np.roll(eye, -1, 1))
    right = np.zeros((line_length, line_length))
    cells = np.arange(line_length)
    for offset, value in (
        (1, 0.5 * COMPACT_NEAR),
        (-1, -0.5 * COMPACT_NEAR),
        (2, 0.25 * COMPACT_FAR),
        (-2, -0.25 * COMPACT_FAR),
    ):
        right[cells, (cells + offset) % line_length] += value
    row = np.linalg.solve(system, right)[0]

    def coef(offset):
        return row[offset % line_length]

    ratio = (-1.0 + np.sqrt(1.0 - 4.0 * COMPACT_ALPHA**2)) / (2.0 * COMPACT_ALPHA)
    gain = coef(NEAR_HALO + 1) / ratio ** (NEAR_HALO + 1)
    n, h = x_cells, NEAR_HALO
    own = np.arange(n)
    send = np.zeros((2 * h + 4, n))
    for k in range(h):
        send[k, n - h + k] = 1.0
    send[h, : n - h] = ratio ** (n - own[: n - h])
    send[h + 1] = ratio ** (2 * n - own)
    for k in range(h):
        send[h + 2 + k, k] = 1.0
    send[2 * h + 2, h:] = ratio ** own[h:]
    send[2 * h + 3] = ratio ** (n + own)
    width = n + 2 * h + 4
    take = np.zeros((n, width))
    for i in range(n):
        take[i, 0] = -gain * ratio**i
        for k in range(h):
            take[i, 1 + k] = coef(-h + k - i)
        take[i, 1 + h] = -gain * ratio**i
        for m in range(n):
            take[i, 2 + h + m] = coef(m - i)
        for k in range(h):
            take[i, 2 + h + n + k] = coef(n + k - i)
        take[i, 2 + 2 * h + n] = gain * ratio ** (n - i)
        take[i, 3 + 2 * h + n] = gain * ratio ** (n - i)
    return send, take


def derive_x(fields):
    x_cells = fields.shape[2]
    groups = lax.axis_size("gx")
    h = NEAR_HALO
    send, take = compact_tables(x_cells, x_cells * groups)
    send = jnp.asarray(send, jnp.float32)
    take = jnp.asarray(take, jnp.float32)
    planes = jnp.einsum("pj,fzjy->fzpy", send, fields, precision=NETWORK_PRECISION)
    to_right = planes[:, :, : h + 1]
    to_right2 = planes[:, :, h + 1 : h + 2]
    to_left = planes[:, :, h + 2 : 2 * h + 3]
    to_left2 = planes[:, :, 2 * h + 3 :]
    from_left = from_behind(to_right, "gx", 1)
    from_left2 = from_behind(to_right2, "gx", 2)
    from_right = from_behind(to_left, "gx", -1)
    from_right2 = from_behind(to_left2, "gx", -2)
    received = jnp.concatenate([from_left2, from_left, from_right, from_right2], axis=2)
    take_own = take[:, h + 2 : h + 2 + x_cells]
    take_received = jnp.concatenate([take[:, : h + 2], take[:, h + 2 + x_cells :]], axis=1)
    own_part = jnp.einsum("ij,fzjy->fziy", take_own, fields, precision=NETWORK_PRECISION)
    return own_part + jnp.einsum(
        "ij,fzjy->fziy", take_received, received, precision=NETWORK_PRECISION
    )


def halo(block, axis, dim, width):
    count = lax.axis_size(axis)
    size = block.shape[dim]
    low_part = lax.slice_in_dim(block, size - width, size, axis=dim)
    high_part = lax.slice_in_dim(block, 0, width, axis=dim)
    if count == 2:
        both = from_behind(jnp.concatenate([low_part, high_part], axis=dim), axis, 1)
        low = lax.slice_in_dim(both, 0, width, axis=dim)
        high = lax.slice_in_dim(both, width, 2 * width, axis=dim)
    else:
        low = from_behind(low_part, axis, 1)
        high = from_behind(high_part, axis, -1)
    return jnp.concatenate([low, block, high], axis=dim)


def centered(extended, along_axis, margin, length):

    def shifted(offset):
        return lax.slice_in_dim(
            extended, margin + offset, margin + offset + length, axis=along_axis
        )

    return (
        45.0 * (shifted(1) - shifted(-1))
        - 9.0 * (shifted(2) - shifted(-2))
        + (shifted(3) - shifted(-3))
    ) / 60.0


def derive_y(fields):
    return centered(halo(fields, "gy", 3, 3), 3, 3, fields.shape[3])


def derive_z(fields):
    return centered(halo(fields, "gz", 1, 3), 1, 3, fields.shape[1])


def butterfly_sum(value, axis):
    count = lax.axis_size(axis)
    step = 1
    while step < count:
        if count % (2 * step) == 0:
            pairs = [(s, s ^ step) for s in range(count)]
            value = value + lax.ppermute(value, axis, pairs)
            step *= 2
        else:
            return lax.psum(value, axis)
    return value


def local(
    mass_per_volume, flow_speed, pressure, cotangent, weight_inner, weight_middle, weight_outer
):
    (state_now, scalars), prepare_pullback = jax.vjp(prepare, mass_per_volume, flow_speed, pressure)
    count = scalars.shape[0]
    first = jnp.concatenate([scalars, cotangent], 0)
    first_x = derive_x(first)
    first_y = derive_y(first)
    first_z = derive_z(first)
    gradients = jnp.stack([first_x[:count], first_y[:count], first_z[:count]])
    spread = jnp.stack([first_x[count:], first_y[count:], first_z[count:]])
    flux_all, flux_pullback = jax.vjp(
        local_flux,
        mass_per_volume,
        flow_speed,
        pressure,
        gradients,
        weight_inner,
        weight_middle,
        weight_outer,
    )
    pulled = flux_pullback(TIME_STEP * spread)
    gradient_bar = pulled[3]
    second_x = derive_x(jnp.concatenate([flux_all[0], gradient_bar[0]], 0))
    second_y = derive_y(jnp.concatenate([flux_all[1], gradient_bar[1]], 0))
    second_z = derive_z(jnp.concatenate([flux_all[2], gradient_bar[2]], 0))
    second = second_x + second_y + second_z
    states = state_now.shape[0]
    state_next = state_now - TIME_STEP * second[:states]
    scalar_bar = -second[states:]
    direct = prepare_pullback((cotangent, scalar_bar))
    weights = (pulled[4], pulled[5], pulled[6])
    flat = jnp.concatenate([w.reshape(-1) for w in weights])
    for axis in ("gz", "gy", "gx"):
        flat = butterfly_sum(flat, axis)
    cells_all = (
        mass_per_volume.size * lax.axis_size("gx") * lax.axis_size("gy") * lax.axis_size("gz")
    )
    factor = 1.0 / math.sqrt(cells_all)
    totals = []
    start = 0
    for w in weights:
        totals.append(flat[start : start + w.size].reshape(w.shape) * factor)
        start += w.size
    return (
        state_next,
        direct[0] + pulled[0],
        direct[1] + pulled[1],
        direct[2] + pulled[2],
        totals[0],
        totals[1],
        totals[2],
    )


def solution(mesh):
    placed = (
        P("gz", "gx", "gy"),
        P(None, "gz", "gx", "gy"),
        P("gz", "gx", "gy"),
        P(None, "gz", "gx", "gy"),
        P(),
        P(),
        P(),
    )
    return jax.shard_map(
        local,
        mesh=mesh,
        in_specs=placed,
        out_specs=(
            P(None, "gz", "gx", "gy"),
            P("gz", "gx", "gy"),
            P(None, "gz", "gx", "gy"),
            P("gz", "gx", "gy"),
            P(),
            P(),
            P(),
        ),
        check_vma=False,
    )
```
